32 devices in a mesh: row: 16 (over z, y, x), col: 2 (over core).
Axes of the slice: x: 2, y: 2, z: 4, core: 2. Of those that a mesh axis runs over, the one named last changes fastest.
Arguments:
- matrix: bfloat16 [16384, 2048], P('row', 'col'), may hold values from -6 to 6
- fill_mask: int32 [64, 16], P('row', 'col'), may hold values from 0 to 1, as said below
- col_rows: int32 [16], replicated, may hold values from 0 to 127, as said below
- inverses: bfloat16 [2, 128, 128], replicated, may hold values from -0.05 to 0.15625
Outputs:
- factor: bfloat16 [16384, 2048], P('row', 'col')
The draws below stay inside these ranges and needn't reach their ends.
Inputs may be any that keep to these rules, and one draw needn't show every extreme that they name: `fill_mask`: each column panel's density of filled blocks is drawn for that column from 1/8 to 8/8. `col_rows`: exactly 1 entries lie in each aligned run of 8 slabs.
All inputs are finite; a program needn't handle non-finite values.
Results may differ from the reference program's by a relative error of at most 0.0035.
Values may be sent and summed in bfloat16 or wider, within the bound.
No kernel may reach another device: no remote copies, remote signals or barrier semaphores. Data moves between devices by JAX's collectives and lax.ppermute only.
A program may use at most 64 MiB of HBM per device.

```python
import jax
import jax.numpy as jnp
from jax import lax

RB = 256
PW = 128
BR_DEV = 4
CP_DEV = 8
NBR = 64
NCP = 16


def draw_fill_mask(key, part):
    key_density, key_cell = jax.random.split(key)
    density = jax.random.randint(key_density, (1, NCP), 1, 9)
    cell_draw = jax.random.randint(key_cell, (NBR, NCP), 0, 8)
    return (cell_draw < density).astype(jnp.int32)


def draw_col_rows(key, part):
    key_perm, key_place = jax.random.split(key)
    row_count = NBR // BR_DEV
    per_device = BR_DEV * RB // PW
    order_draw = jax.random.permutation(key_perm, NCP)
    owner_row = order_draw % row_count
    slab_place = jax.random.randint(key_place, (NCP,), 0, per_device)
    slab_place = jnp.where(order_draw == NCP - 1, per_device - 1, jnp.where(order_draw == 0, 0, slab_place))
    return (owner_row * per_device + slab_place).astype(jnp.int32)


def draw_inverses(key, part):
    key_diag, key_off = jax.random.split(jax.random.fold_in(key, 7))
    diag_vals = jax.random.uniform(key_diag, (2, PW), jnp.float32, 0.1, 0.15625)
    off_vals = 0.01 * jax.random.normal(key_off, (2, PW, PW), jnp.float32)
    off_vals = jnp.clip(off_vals, -0.05, 0.05)
    eye_table = (jnp.arange(PW)[:, None] == jnp.arange(PW)[None, :]).astype(jnp.float32)
    result = diag_vals[:, :, None] * eye_table[None, :, :] + off_vals * (1.0 - eye_table[None, :, :])
    return result.astype(jnp.bfloat16)


def block_levels(own_key, extent, cuts, smallest, high):
    level, own = 1.0, jax.random.fold_in(own_key, 6)
    for position, blocks in cuts:
        steps = jnp.exp(jax.random.uniform(jax.random.fold_in(own, position), (blocks,), jnp.float32, smallest / len(cuts), high / len(cuts)))
        level = level * jnp.repeat(steps, extent[position] // blocks).reshape([-1 if axis == position else 1 for axis in range(len(extent))])
    return level


def gaussian(key, dims, scale, reach, cuts=(), held_as=jnp.bfloat16):
    gain = block_levels(key, dims, cuts, -0.22, 0.18) if cuts else 1.0
    array = jax.random.normal(key, dims, jnp.float32) * scale * gain
    return jnp.minimum(jnp.maximum(array, -reach), reach).astype(held_as)


def setup_inputs(seed: int = 0) -> dict:
    keys = jax.random.split(jax.random.key(seed), 5)
    matrix = gaussian(keys[0], (NBR * RB, NCP * PW), 1.0, 6.0, ((0, 16), (1, 2)))
    fill_mask = draw_fill_mask(jax.random.fold_in(keys[4], 71), 0)
    col_rows = draw_col_rows(jax.random.fold_in(keys[4], 71), 0)
    inverses = draw_inverses(jax.random.fold_in(keys[4], 71), 0)
    return {"matrix": matrix, "fill_mask": fill_mask, "col_rows": col_rows, "inverses": inverses}


def contract(left, right):
    return lax.dot_general(left, right, (((1,), (1,)), ((), ())), preferred_element_type=jnp.float32)


def reference(matrix, fill_mask, col_rows, inverses):
    rows_mask = jnp.repeat(fill_mask.astype(jnp.float32), RB, axis=0)
    upper_first = jnp.triu(inverses[0])
    upper_second = jnp.triu(inverses[1])
    first_panel = (jnp.dot(matrix[:, :PW], upper_first, preferred_element_type=jnp.float32) * rows_mask[:, 0:1]).astype(jnp.bfloat16)
    diag_first = first_panel.reshape(-1, PW, PW)[col_rows]
    second_col = matrix[:, CP_DEV * PW:(CP_DEV + 1) * PW]
    panel_update = (second_col.astype(jnp.float32) - contract(first_panel, diag_first[CP_DEV])).astype(jnp.bfloat16)
    second_panel = (jnp.dot(panel_update, upper_second, preferred_element_type=jnp.float32) * rows_mask[:, CP_DEV:CP_DEV + 1]).astype(jnp.bfloat16)
    diag_second = second_panel.reshape(-1, PW, PW)[col_rows]

    def column_tile(column):
        col_block = lax.dynamic_slice_in_dim(matrix, column * PW, PW, 1)
        schur_sum = col_block.astype(jnp.float32) - contract(first_panel, diag_first[column])
        schur_sum = schur_sum - contract(second_panel, diag_second[column])
        masked = (schur_sum * rows_mask[:, column][:, None]).astype(jnp.bfloat16)
        masked = jnp.where(column == 0, first_panel, masked)
        return jnp.where(column == CP_DEV, second_panel, masked)

    tile_stack = lax.map(column_tile, jnp.arange(NCP, dtype=jnp.int32))
    return jnp.transpose(tile_stack, (1, 0, 2)).reshape(NBR * RB, NCP * PW)
```

```python
import jax
import jax.numpy as jnp
from jax import lax
from jax.sharding import PartitionSpec as P

RB = 256
PW = 128
FIRST_COL = 0
SECOND_COL = 1
MASK_ROWS = 16


def contract(left, right):
    return lax.dot_general(
        left, right, (((1,), (1,)), ((), ())), preferred_element_type=jnp.float32
    )


def lead_columns(payload):
    col_count = lax.axis_size("col")
    if col_count == 2:
        other = lax.ppermute(payload, "col", [(0, 1), (1, 0)])
        first = lax.axis_index("col") == FIRST_COL
        return jnp.where(first, payload, other), jnp.where(first, other, payload)
    gathered = lax.all_gather(payload, "col", axis=0, tiled=False)
    return gathered[FIRST_COL], gathered[SECOND_COL]


def gather_rows(piece):
    row_count = lax.axis_size("row")
    me = lax.axis_index("row")
    bits = row_count.bit_length() - 1
    if (1 << bits) != row_count:
        everyone = lax.all_gather(piece, "row", axis=0, tiled=False)
        return everyone, lambda owner: owner
    held = piece[None]
    order = list(range(bits))[::-1]
    for bit in order:
        step = 1 << bit
        perm = [(i, i ^ step) for i in range(row_count)]
        held = jnp.concatenate((held, lax.ppermute(held, "row", perm)), axis=0)

    def slot_of(owner):
        diff = jnp.bitwise_xor(owner, me)
        slot = jnp.zeros_like(diff)
        for position, bit in enumerate(order):
            slot = slot + ((diff >> bit) & 1) * (1 << position)
        return slot

    return held, slot_of


def shards(matrix, fill_mask, col_rows, inverses):
    col_index = lax.axis_index("col")
    row_index = lax.axis_index("row")
    local_rows, width = matrix.shape
    col_panels = width // PW
    block_rows = local_rows // RB
    local_slabs = local_rows // PW
    upper_first = jnp.triu(inverses[0])
    upper_second = jnp.triu(inverses[1])

    mask_f = fill_mask.astype(jnp.bfloat16)
    mask_rows = jnp.zeros((MASK_ROWS, PW), jnp.bfloat16)
    mask_rows = mask_rows.at[:block_rows].set(jnp.broadcast_to(mask_f[:, 0:1], (block_rows, PW)))
    payload = jnp.concatenate((matrix[:, :PW], mask_rows), axis=0)
    first_cols, second_cols = lead_columns(payload)

    owner_row = col_rows // local_slabs
    slab_place = col_rows % local_slabs
    owned = owner_row == row_index
    place = jnp.sum(jnp.where(owned, slab_place, 0))
    block = place // (RB // PW)
    first_slab = lax.dynamic_slice_in_dim(first_cols, place * PW, PW, 0)
    second_slab = lax.dynamic_slice_in_dim(second_cols, place * PW, PW, 0)
    first_flag = lax.dynamic_slice_in_dim(first_cols, local_rows + block, 1, 0)
    second_flag = lax.dynamic_slice_in_dim(second_cols, local_rows + block, 1, 0)
    flags = jnp.concatenate(
        (first_flag, second_flag, jnp.zeros((MASK_ROWS - 2, PW), jnp.bfloat16)), axis=0
    )
    piece = jnp.concatenate((first_slab, second_slab, flags), axis=0)
    held, slot_of = gather_rows(piece)

    wanted = col_index * col_panels + jnp.arange(col_panels, dtype=jnp.int32)
    wanted = jnp.concatenate((wanted, jnp.full((1,), SECOND_COL * col_panels, jnp.int32)))
    slots = slot_of(owner_row[wanted])
    pick = (slots[:, None] == jnp.arange(held.shape[0], dtype=jnp.int32)[None, :]).astype(
        jnp.bfloat16
    )
    picked = jnp.einsum(
        "tq,qij->tij", pick, held, preferred_element_type=jnp.float32
    ).astype(jnp.bfloat16)
    slab_first = picked[:, :PW]
    slab_second = picked[:, PW : 2 * PW]
    flag_first = picked[:, 2 * PW, 0].astype(jnp.float32)
    flag_second = picked[:, 2 * PW + 1, 0].astype(jnp.float32)

    diag_first = (
        jnp.einsum("tij,jk->tik", slab_first, upper_first, preferred_element_type=jnp.float32)
        * flag_first[:, None, None]
    ).astype(jnp.bfloat16)
    pivot = diag_first[col_panels]
    diag_update = (
        slab_second.astype(jnp.float32)
        - jnp.einsum("tij,kj->tik", diag_first, pivot, preferred_element_type=jnp.float32)
    ).astype(jnp.bfloat16)
    diag_second = (
        jnp.einsum("tij,jk->tik", diag_update, upper_second, preferred_element_type=jnp.float32)
        * flag_second[:, None, None]
    ).astype(jnp.bfloat16)

    rows_first = jnp.repeat(first_cols[local_rows : local_rows + block_rows, 0:1], RB, axis=0)
    rows_second = jnp.repeat(second_cols[local_rows : local_rows + block_rows, 0:1], RB, axis=0)
    first_panel = (
        jnp.dot(first_cols[:local_rows], upper_first, preferred_element_type=jnp.float32)
        * rows_first.astype(jnp.float32)
    ).astype(jnp.bfloat16)
    panel_update = (
        second_cols[:local_rows].astype(jnp.float32) - contract(first_panel, pivot)
    ).astype(jnp.bfloat16)
    second_panel = (
        jnp.dot(panel_update, upper_second, preferred_element_type=jnp.float32)
        * rows_second.astype(jnp.float32)
    ).astype(jnp.bfloat16)

    both_panels = jnp.concatenate((first_panel, second_panel), axis=1)
    both_diag = jnp.concatenate(
        (diag_first[:col_panels], diag_second[:col_panels]), axis=2
    ).reshape(-1, 2 * PW)
    schur_sum = matrix.astype(jnp.float32) - contract(both_panels, both_diag)
    rows_mask = jnp.repeat(fill_mask.astype(jnp.float32), RB, axis=0)
    masked = (
        (schur_sum.reshape(local_rows, col_panels, PW) * rows_mask[:, :, None])
        .astype(jnp.bfloat16)
        .reshape(local_rows, width)
    )
    leading = jnp.where(
        col_index == FIRST_COL,
        first_panel,
        jnp.where(col_index == SECOND_COL, second_panel, masked[:, :PW]),
    )
    return jnp.concatenate((leading, masked[:, PW:]), axis=1)


def solution(mesh):
    in_specs = (P("row", "col"), P("row", "col"), P(), P())
    out_specs = P("row", "col")
    return jax.shard_map(shards, mesh=mesh, in_specs=in_specs, out_specs=out_specs, check_vma=False)
```

```python
import jax
import jax.numpy as jnp
from jax import lax
from jax.sharding import PartitionSpec as P

RB = 256
PW = 128
FIRST_COL = 0
SECOND_COL = 1
MASK_ROWS = 16


def contract(left, right):
    return lax.dot_general(
        left, right, (((1,), (1,)), ((), ())), preferred_element_type=jnp.float32
    )


def round_orders(bits):
    even = list(range(bits))[::-1]
    odd = list(even)
    for position in range(0, bits - 1, 2):
        odd[position], odd[position + 1] = odd[position + 1], odd[position]
    return even, odd


def gather_rows(piece, row_count, col_count):
    me = lax.axis_index("row")
    parity = lax.axis_index("col") % 2
    bits = row_count.bit_length() - 1
    even, odd = round_orders(bits)
    held = piece[None]
    for step in range(bits):
        perm = []
        for r in range(row_count):
            for k in range(col_count):
                bit = (even if k % 2 == 0 else odd)[step]
                perm.append((r * col_count + k, (r ^ (1 << bit)) * col_count + k))
        held = jnp.concatenate((held, lax.ppermute(held, ("row", "col"), perm)), axis=0)

    def slot_of(owner, order_parity):
        diff = jnp.bitwise_xor(owner, me)
        slot_even = jnp.zeros_like(diff)
        slot_odd = jnp.zeros_like(diff)
        for position in range(bits):
            slot_even = slot_even + ((diff >> even[position]) & 1) * (1 << position)
            slot_odd = slot_odd + ((diff >> odd[position]) & 1) * (1 << position)
        return jnp.where(order_parity == 0, slot_even, slot_odd)

    return held, slot_of, parity


def shards(matrix, fill_mask, col_rows, inverses):
    col_index = lax.axis_index("col")
    row_index = lax.axis_index("row")
    row_count = lax.axis_size("row")
    col_count = lax.axis_size("col")
    local_rows, width = matrix.shape
    col_panels = width // PW
    block_rows = local_rows // RB
    local_slabs = local_rows // PW
    upper_first = jnp.triu(inverses[0])
    upper_second = jnp.triu(inverses[1])
    mask_f = fill_mask.astype(jnp.bfloat16)

    owner_row = col_rows // local_slabs
    slab_place = col_rows % local_slabs
    place = jnp.sum(jnp.where(owner_row == row_index, slab_place, 0))
    block = place // (RB // PW)
    own_slab = lax.dynamic_slice_in_dim(matrix[:, :PW], place * PW, PW, 0)
    own_flag = lax.dynamic_slice_in_dim(mask_f[:, 0:1], block, 1, 0)
    flag_rows = jnp.zeros((MASK_ROWS, PW), jnp.bfloat16).at[0:1].set(
        jnp.broadcast_to(own_flag, (1, PW))
    )
    piece = jnp.concatenate((own_slab, flag_rows), axis=0)
    held, slot_of, parity = gather_rows(piece, row_count, col_count)

    mask_rows = jnp.zeros((MASK_ROWS, PW), jnp.bfloat16)
    mask_rows = mask_rows.at[:block_rows].set(jnp.broadcast_to(mask_f[:, 0:1], (block_rows, PW)))
    payload = jnp.concatenate((matrix[:, :PW], mask_rows), axis=0)

    def wanted_of(group):
        own = group * col_panels + jnp.arange(col_panels, dtype=jnp.int32)
        return jnp.concatenate((own, jnp.full((1,), SECOND_COL * col_panels, jnp.int32)))

    def pick(pieces, wanted, order_parity):
        slots = slot_of(owner_row[wanted], order_parity)
        return jnp.take(pieces, slots, axis=0)

    wanted = wanted_of(col_index)
    if col_count == 2:
        swap = [(0, 1), (1, 0)]
        other = lax.ppermute(payload, "col", swap)
        first = col_index == FIRST_COL
        first_cols = jnp.where(first, payload, other)
        second_cols = jnp.where(first, other, payload)
        mine = pick(held, wanted, parity)
        for_partner = pick(held, wanted_of(1 - col_index), parity)
        theirs = lax.ppermute(for_partner, "col", swap)
        pieces_first = jnp.where(first, mine, theirs)
        pieces_second = jnp.where(first, theirs, mine)
    else:
        lead = lax.all_gather(payload, "col", axis=0, tiled=False)
        first_cols, second_cols = lead[FIRST_COL], lead[SECOND_COL]
        everyone = lax.all_gather(held, "col", axis=0, tiled=False)
        pieces_first = pick(everyone[FIRST_COL], wanted, FIRST_COL % 2)
        pieces_second = pick(everyone[SECOND_COL], wanted, SECOND_COL % 2)

    slab_first = pieces_first[:, :PW]
    slab_second = pieces_second[:, :PW]
    flag_first = pieces_first[:, PW, 0].astype(jnp.float32)
    flag_second = pieces_second[:, PW, 0].astype(jnp.float32)

    diag_first = (
        jnp.einsum("tij,jk->tik", slab_first, upper_first, preferred_element_type=jnp.float32)
        * flag_first[:, None, None]
    ).astype(jnp.bfloat16)
    pivot = diag_first[col_panels]
    diag_update = (
        slab_second.astype(jnp.float32)
        - jnp.einsum("tij,kj->tik", diag_first, pivot, preferred_element_type=jnp.float32)
    ).astype(jnp.bfloat16)
    diag_second = (
        jnp.einsum("tij,jk->tik", diag_update, upper_second, preferred_element_type=jnp.float32)
        * flag_second[:, None, None]
    ).astype(jnp.bfloat16)

    rows_first = jnp.repeat(first_cols[local_rows : local_rows + block_rows, 0:1], RB, axis=0)
    rows_second = jnp.repeat(second_cols[local_rows : local_rows + block_rows, 0:1], RB, axis=0)
    first_panel = (
        jnp.dot(first_cols[:local_rows], upper_first, preferred_element_type=jnp.float32)
        * rows_first.astype(jnp.float32)
    ).astype(jnp.bfloat16)
    panel_update = (
        second_cols[:local_rows].astype(jnp.float32) - contract(first_panel, pivot)
    ).astype(jnp.bfloat16)
    second_panel = (
        jnp.dot(panel_update, upper_second, preferred_element_type=jnp.float32)
        * rows_second.astype(jnp.float32)
    ).astype(jnp.bfloat16)

    both_panels = jnp.concatenate((first_panel, second_panel), axis=1)
    both_diag_t = jnp.concatenate(
        (
            jnp.transpose(diag_first[:col_panels], (2, 0, 1)),
            jnp.transpose(diag_second[:col_panels], (2, 0, 1)),
        ),
        axis=0,
    ).reshape(2 * PW, width)
    schur_sum = matrix.astype(jnp.float32) - jnp.dot(
        both_panels, both_diag_t, preferred_element_type=jnp.float32
    )
    rows_mask = jnp.repeat(fill_mask.astype(jnp.float32), RB, axis=0)
    masked = (
        (schur_sum.reshape(local_rows, col_panels, PW) * rows_mask[:, :, None])
        .astype(jnp.bfloat16)
        .reshape(local_rows, width)
    )
    leading = jnp.where(
        col_index == FIRST_COL,
        first_panel,
        jnp.where(col_index == SECOND_COL, second_panel, masked[:, :PW]),
    )
    return jnp.concatenate((leading, masked[:, PW:]), axis=1)


def solution(mesh):
    in_specs = (P("row", "col"), P("row", "col"), P(), P())
    out_specs = P("row", "col")
    return jax.shard_map(shards, mesh=mesh, in_specs=in_specs, out_specs=out_specs, check_vma=False)
```

```python
import jax
import jax.numpy as jnp
from jax import lax
from jax.experimental import pallas as pl
from jax.experimental.pallas import tpu as pltpu
from jax.sharding import PartitionSpec as P

RB = 256
PW = 128
FIRST_COL = 0
SECOND_COL = 1
MASK_ROWS = 16


def round_orders(bits):
    even = list(range(bits))[::-1]
    odd = list(even)
    for position in range(0, bits - 1, 2):
        odd[position], odd[position + 1] = odd[position + 1], odd[position]
    return even, odd


def gather_rows(piece, row_count, col_count):
    me = lax.axis_index("row")
    parity = lax.axis_index("col") % 2
    bits = row_count.bit_length() - 1
    even, odd = round_orders(bits)
    held = piece[None]
    for step in range(bits):
        perm = []
        for r in range(row_count):
            for k in range(col_count):
                bit = (even if k % 2 == 0 else odd)[step]
                perm.append((r * col_count + k, (r ^ (1 << bit)) * col_count + k))
        held = jnp.concatenate((held, lax.ppermute(held, ("row", "col"), perm)), axis=0)

    def slot_of(owner, order_parity):
        diff = jnp.bitwise_xor(owner, me)
        slot_even = jnp.zeros_like(diff)
        slot_odd = jnp.zeros_like(diff)
        for position in range(bits):
            slot_even = slot_even + ((diff >> even[position]) & 1) * (1 << position)
            slot_odd = slot_odd + ((diff >> odd[position]) & 1) * (1 << position)
        return jnp.where(order_parity == 0, slot_even, slot_odd)

    return held, slot_of, parity


def shards(matrix, fill_mask, col_rows, inverses):
    col_index = lax.axis_index("col")
    row_index = lax.axis_index("row")
    row_count = lax.axis_size("row")
    col_count = lax.axis_size("col")
    local_rows, width = matrix.shape
    col_panels = width // PW
    block_rows = local_rows // RB
    local_slabs = local_rows // PW
    mask_f = fill_mask.astype(jnp.bfloat16)

    owner_row = col_rows // local_slabs
    slab_place = col_rows % local_slabs
    place = jnp.sum(jnp.where(owner_row == row_index, slab_place, 0))
    block = place // (RB // PW)
    own_slab = lax.dynamic_slice_in_dim(matrix[:, :PW], place * PW, PW, 0)
    own_flag = lax.dynamic_slice_in_dim(mask_f[:, 0:1], block, 1, 0)
    flag_rows = jnp.zeros((MASK_ROWS, PW), jnp.bfloat16).at[0:1].set(
        jnp.broadcast_to(own_flag, (1, PW))
    )
    piece = jnp.concatenate((own_slab, flag_rows), axis=0)
    held, slot_of, parity = gather_rows(piece, row_count, col_count)

    mask_rows = jnp.zeros((MASK_ROWS, PW), jnp.bfloat16)
    mask_rows = mask_rows.at[:block_rows].set(jnp.broadcast_to(mask_f[:, 0:1], (block_rows, PW)))
    payload = jnp.concatenate((matrix[:, :PW], mask_rows), axis=0)

    def wanted_of(group):
        own = group * col_panels + jnp.arange(col_panels, dtype=jnp.int32)
        return jnp.concatenate((own, jnp.full((1,), SECOND_COL * col_panels, jnp.int32)))

    def pick(pieces, wanted, order_parity):
        slots = slot_of(owner_row[wanted], order_parity)
        return jnp.take(pieces, slots, axis=0)

    wanted = wanted_of(col_index)
    if col_count == 2:
        swap = [(0, 1), (1, 0)]
        cols_a = payload
        cols_b = lax.ppermute(payload, "col", swap)
        pieces_a = pick(held, wanted, parity)
        for_partner = pick(held, wanted_of(1 - col_index), parity)
        pieces_b = lax.ppermute(for_partner, "col", swap)
        order = col_index
    else:
        lead = lax.all_gather(payload, "col", axis=0, tiled=False)
        cols_a, cols_b = lead[FIRST_COL], lead[SECOND_COL]
        everyone = lax.all_gather(held, "col", axis=0, tiled=False)
        pieces_a = pick(everyone[FIRST_COL], wanted, FIRST_COL % 2)
        pieces_b = pick(everyone[SECOND_COL], wanted, SECOND_COL % 2)
        order = jnp.zeros_like(col_index)

    table = jnp.stack((order, col_index)).astype(jnp.int32)
    return factor_call(
        matrix, cols_a, cols_b, pieces_a, pieces_b, inverses, fill_mask, table
    )


def factor_kernel(
    matrix_ref, cols_a_ref, cols_b_ref, pieces_a_ref, pieces_b_ref, inv_ref, mask_ref, table_ref, out_ref
):
    local_rows, width = matrix_ref.shape
    col_panels = width // PW
    block_rows = local_rows // RB
    picks = pieces_a_ref.shape[0]
    swapped = table_ref[0] != 0
    col_index = table_ref[1]

    def dot(left, right):
        return jnp.dot(left, right, preferred_element_type=jnp.float32)

    def dot_t(left, right):
        return lax.dot_general(
            left, right, (((1,), (1,)), ((), ())), preferred_element_type=jnp.float32
        )

    upper = (
        lax.broadcasted_iota(jnp.int32, (PW, PW), 0) <= lax.broadcasted_iota(jnp.int32, (PW, PW), 1)
    )
    zero = jnp.zeros((PW, PW), jnp.bfloat16)
    upper_first = jnp.where(upper, inv_ref[0], zero)
    upper_second = jnp.where(upper, inv_ref[1], zero)

    def first_second(a_ref, b_ref, index):
        a_val, b_val = a_ref[index], b_ref[index]
        return jnp.where(swapped, b_val, a_val), jnp.where(swapped, a_val, b_val)

    diag_first, diag_second = [], []
    for t in range(picks):
        piece_first, piece_second = first_second(pieces_a_ref, pieces_b_ref, t)
        flag_first = piece_first[PW : PW + 1].astype(jnp.float32)
        diag_first.append((dot(piece_first[:PW], upper_first) * flag_first).astype(jnp.bfloat16))
    pivot = diag_first[col_panels]
    for t in range(col_panels):
        piece_first, piece_second = first_second(pieces_a_ref, pieces_b_ref, t)
        flag_second = piece_second[PW : PW + 1].astype(jnp.float32)
        update = (
            piece_second[:PW].astype(jnp.float32) - dot_t(diag_first[t], pivot)
        ).astype(jnp.bfloat16)
        diag_second.append((dot(update, upper_second) * flag_second).astype(jnp.bfloat16))
    both_diag = [
        jnp.concatenate((diag_first[t], diag_second[t]), axis=1) for t in range(col_panels)
    ]

    for b in range(block_rows):
        rows = slice(b * RB, (b + 1) * RB)
        cols_first, cols_second = first_second(cols_a_ref, cols_b_ref, rows)
        flags_first, flags_second = first_second(
            cols_a_ref, cols_b_ref, slice(local_rows + b, local_rows + b + 1)
        )
        first_panel = (dot(cols_first, upper_first) * flags_first.astype(jnp.float32)).astype(
            jnp.bfloat16
        )
        panel_update = (
            cols_second.astype(jnp.float32) - dot_t(first_panel, pivot)
        ).astype(jnp.bfloat16)
        second_panel = (
            dot(panel_update, upper_second) * flags_second.astype(jnp.float32)
        ).astype(jnp.bfloat16)
        both_panels = jnp.concatenate((first_panel, second_panel), axis=1)
        for j in range(col_panels):
            cols = slice(j * PW, (j + 1) * PW)
            schur = matrix_ref[rows, cols].astype(jnp.float32) - dot_t(both_panels, both_diag[j])
            tile = (schur * mask_ref[b, j].astype(jnp.float32)).astype(jnp.bfloat16)
            if j == 0:
                tile = jnp.where(
                    col_index == FIRST_COL,
                    first_panel,
                    jnp.where(col_index == SECOND_COL, second_panel, tile),
                )
            out_ref[rows, cols] = tile


def factor_call(matrix, cols_a, cols_b, pieces_a, pieces_b, inverses, fill_mask, table):
    local_rows, width = matrix.shape
    vmem = pl.BlockSpec(memory_space=pltpu.VMEM)
    smem = pl.BlockSpec(memory_space=pltpu.SMEM)
    flops = 2 * local_rows * width * 2 * PW + 6 * local_rows * PW * PW
    return pl.pallas_call(
        factor_kernel,
        out_shape=jax.ShapeDtypeStruct((local_rows, width), jnp.bfloat16),
        in_specs=[vmem] * 6 + [smem, smem],
        out_specs=vmem,
        cost_estimate=pl.CostEstimate(
            flops=flops, bytes_accessed=4 * local_rows * width, transcendentals=0
        ),
    )(matrix, cols_a, cols_b, pieces_a, pieces_b, inverses, fill_mask, table)


def solution(mesh):
    in_specs = (P("row", "col"), P("row", "col"), P(), P())
    out_specs = P("row", "col")
    return jax.shard_map(shards, mesh=mesh, in_specs=in_specs, out_specs=out_specs, check_vma=False)
```

```python
import jax
import jax.numpy as jnp
from jax import lax
from jax.experimental import pallas as pl
from jax.experimental.pallas import tpu as pltpu
from jax.sharding import PartitionSpec as P

RB = 256
PW = 128
FIRST_COL = 0
SECOND_COL = 1
MASK_ROWS = 16


def round_orders(bits):
    even = list(range(bits))[::-1]
    odd = list(even)
    for position in range(0, bits - 1, 2):
        odd[position], odd[position + 1] = odd[position + 1], odd[position]
    return even, odd


def gather_rows(piece, row_count, col_count):
    me = lax.axis_index("row")
    parity = lax.axis_index("col") % 2
    bits = row_count.bit_length() - 1
    even, odd = round_orders(bits)
    held = piece[None]
    for step in range(bits):
        perm = []
        for r in range(row_count):
            for k in range(col_count):
                bit = (even if k % 2 == 0 else odd)[step]
                perm.append((r * col_count + k, (r ^ (1 << bit)) * col_count + k))
        held = jnp.concatenate((held, lax.ppermute(held, ("row", "col"), perm)), axis=0)

    def slot_of(owner, order_parity):
        diff = jnp.bitwise_xor(owner, me)
        slot_even = jnp.zeros_like(diff)
        slot_odd = jnp.zeros_like(diff)
        for position in range(bits):
            slot_even = slot_even + ((diff >> even[position]) & 1) * (1 << position)
            slot_odd = slot_odd + ((diff >> odd[position]) & 1) * (1 << position)
        return jnp.where(order_parity == 0, slot_even, slot_odd)

    return held, slot_of, parity


def shards(matrix, fill_mask, col_rows, inverses):
    col_index = lax.axis_index("col")
    row_index = lax.axis_index("row")
    row_count = lax.axis_size("row")
    col_count = lax.axis_size("col")
    local_rows, width = matrix.shape
    col_panels = width // PW
    block_rows = local_rows // RB
    local_slabs = local_rows // PW
    mask_f = fill_mask.astype(jnp.bfloat16)

    owner_row = col_rows // local_slabs
    local_ids = row_index * local_slabs + jnp.arange(local_slabs, dtype=jnp.int32)
    choose = jnp.sum((col_rows[None, :] == local_ids[:, None]).astype(jnp.int32), axis=1)
    choose_f = choose.astype(jnp.bfloat16)
    own_slab = jnp.einsum(
        "s,sij->ij",
        choose_f,
        matrix[:, :PW].reshape(local_slabs, PW, PW),
        preferred_element_type=jnp.float32,
    ).astype(jnp.bfloat16)
    slab_mask = jnp.repeat(fill_mask[:, 0], RB // PW).astype(jnp.bfloat16)
    flag_block = jnp.where(
        lax.broadcasted_iota(jnp.int32, (local_slabs, MASK_ROWS, PW), 1) == 0,
        slab_mask[:, None, None],
        jnp.bfloat16(0),
    )
    flag_rows = jnp.einsum(
        "s,sij->ij", choose_f, flag_block, preferred_element_type=jnp.float32
    ).astype(jnp.bfloat16)
    piece = jnp.concatenate((own_slab, flag_rows), axis=0)
    held, slot_of, parity = gather_rows(piece, row_count, col_count)

    mask_rows = jnp.zeros((MASK_ROWS, PW), jnp.bfloat16)
    mask_rows = mask_rows.at[:block_rows].set(jnp.broadcast_to(mask_f[:, 0:1], (block_rows, PW)))
    payload = jnp.concatenate((matrix[:, :PW], mask_rows), axis=0)

    def wanted_of(group):
        own = group * col_panels + jnp.arange(col_panels, dtype=jnp.int32)
        return jnp.concatenate((own, jnp.full((1,), SECOND_COL * col_panels, jnp.int32)))

    def pick(pieces, wanted, order_parity):
        slots = slot_of(owner_row[wanted], order_parity)
        return jnp.take(pieces, slots, axis=0)

    wanted = wanted_of(col_index)
    if col_count == 2:
        swap = [(0, 1), (1, 0)]
        cols_a = payload
        cols_b = lax.ppermute(payload, "col", swap)
        pieces_a = pick(held, wanted, parity)
        for_partner = pick(held, wanted_of(1 - col_index), parity)
        pieces_b = lax.ppermute(for_partner, "col", swap)
        order = col_index
    else:
        lead = lax.all_gather(payload, "col", axis=0, tiled=False)
        cols_a, cols_b = lead[FIRST_COL], lead[SECOND_COL]
        everyone = lax.all_gather(held, "col", axis=0, tiled=False)
        pieces_a = pick(everyone[FIRST_COL], wanted, FIRST_COL % 2)
        pieces_b = pick(everyone[SECOND_COL], wanted, SECOND_COL % 2)
        order = jnp.zeros_like(col_index)

    table = jnp.stack((order, col_index)).astype(jnp.int32)
    return factor_call(
        matrix, cols_a, cols_b, pieces_a, pieces_b, inverses, fill_mask, table
    )


def factor_kernel(
    matrix_ref, cols_a_ref, cols_b_ref, pieces_a_ref, pieces_b_ref, inv_ref, mask_ref, table_ref, out_ref
):
    local_rows, width = matrix_ref.shape
    col_panels = width // PW
    block_rows = local_rows // RB
    picks = pieces_a_ref.shape[0]
    swapped = table_ref[0] != 0
    col_index = table_ref[1]

    def dot(left, right):
        return jnp.dot(left, right, preferred_element_type=jnp.float32)

    def dot_t(left, right):
        return lax.dot_general(
            left, right, (((1,), (1,)), ((), ())), preferred_element_type=jnp.float32
        )

    upper = (
        lax.broadcasted_iota(jnp.int32, (PW, PW), 0) <= lax.broadcasted_iota(jnp.int32, (PW, PW), 1)
    )
    zero = jnp.zeros((PW, PW), jnp.bfloat16)
    upper_first = jnp.where(upper, inv_ref[0], zero)
    upper_second = jnp.where(upper, inv_ref[1], zero)

    def first_second(a_ref, b_ref, index):
        a_val, b_val = a_ref[index], b_ref[index]
        return jnp.where(swapped, b_val, a_val), jnp.where(swapped, a_val, b_val)

    diag_first, diag_second = [], []
    for t in range(picks):
        piece_first, piece_second = first_second(pieces_a_ref, pieces_b_ref, t)
        flag_first = piece_first[PW : PW + 1].astype(jnp.float32)
        diag_first.append((dot(piece_first[:PW], upper_first) * flag_first).astype(jnp.bfloat16))
    pivot = diag_first[col_panels]
    for t in range(col_panels):
        piece_first, piece_second = first_second(pieces_a_ref, pieces_b_ref, t)
        flag_second = piece_second[PW : PW + 1].astype(jnp.float32)
        update = (
            piece_second[:PW].astype(jnp.float32) - dot_t(diag_first[t], pivot)
        ).astype(jnp.bfloat16)
        diag_second.append((dot(update, upper_second) * flag_second).astype(jnp.bfloat16))
    both_diag = [
        jnp.concatenate((diag_first[t], diag_second[t]), axis=1) for t in range(col_panels)
    ]

    for b in range(block_rows):
        rows = slice(b * RB, (b + 1) * RB)
        cols_first, cols_second = first_second(cols_a_ref, cols_b_ref, rows)
        flags_first, flags_second = first_second(
            cols_a_ref, cols_b_ref, slice(local_rows + b, local_rows + b + 1)
        )
        first_panel = (dot(cols_first, upper_first) * flags_first.astype(jnp.float32)).astype(
            jnp.bfloat16
        )
        panel_update = (
            cols_second.astype(jnp.float32) - dot_t(first_panel, pivot)
        ).astype(jnp.bfloat16)
        second_panel = (
            dot(panel_update, upper_second) * flags_second.astype(jnp.float32)
        ).astype(jnp.bfloat16)
        both_panels = jnp.concatenate((first_panel, second_panel), axis=1)
        for j in range(col_panels):
            cols = slice(j * PW, (j + 1) * PW)
            schur = matrix_ref[rows, cols].astype(jnp.float32) - dot_t(both_panels, both_diag[j])
            tile = (schur * mask_ref[b, j].astype(jnp.float32)).astype(jnp.bfloat16)
            if j == 0:
                tile = jnp.where(
                    col_index == FIRST_COL,
                    first_panel,
                    jnp.where(col_index == SECOND_COL, second_panel, tile),
                )
            out_ref[rows, cols] = tile


def factor_call(matrix, cols_a, cols_b, pieces_a, pieces_b, inverses, fill_mask, table):
    local_rows, width = matrix.shape
    vmem = pl.BlockSpec(memory_space=pltpu.VMEM)
    smem = pl.BlockSpec(memory_space=pltpu.SMEM)
    flops = 2 * local_rows * width * 2 * PW + 6 * local_rows * PW * PW
    return pl.pallas_call(
        factor_kernel,
        out_shape=jax.ShapeDtypeStruct((local_rows, width), jnp.bfloat16),
        in_specs=[vmem] * 6 + [smem, smem],
        out_specs=vmem,
        cost_estimate=pl.CostEstimate(
            flops=flops, bytes_accessed=4 * local_rows * width, transcendentals=0
        ),
    )(matrix, cols_a, cols_b, pieces_a, pieces_b, inverses, fill_mask, table)


def solution(mesh):
    in_specs = (P("row", "col"), P("row", "col"), P(), P())
    out_specs = P("row", "col")
    return jax.shard_map(shards, mesh=mesh, in_specs=in_specs, out_specs=out_specs, check_vma=False)
```

```python
import functools

import jax
import jax.numpy as jnp
from jax import lax
from jax.experimental import pallas as pl
from jax.experimental.pallas import tpu as pltpu
from jax.sharding import PartitionSpec as P

RB = 256
PW = 128
FIRST_COL = 0
SECOND_COL = 1
MASK_ROWS = 16


def round_orders(bits):
    even = list(range(bits))[::-1]
    odd = list(even)
    for position in range(0, bits - 1, 2):
        odd[position], odd[position + 1] = odd[position + 1], odd[position]
    return even, odd


def gather_rows(piece, row_count, col_count):
    me = lax.axis_index("row")
    parity = lax.axis_index("col") % 2
    bits = row_count.bit_length() - 1
    even, odd = round_orders(bits)
    held = piece[None]
    for step in range(bits):
        perm = []
        for r in range(row_count):
            for k in range(col_count):
                bit = (even if k % 2 == 0 else odd)[step]
                perm.append((r * col_count + k, (r ^ (1 << bit)) * col_count + k))
        held = jnp.concatenate((held, lax.ppermute(held, ("row", "col"), perm)), axis=0)

    def slot_of(owner, order_parity):
        diff = jnp.bitwise_xor(owner, me)
        slot_even = jnp.zeros_like(diff)
        slot_odd = jnp.zeros_like(diff)
        for position in range(bits):
            slot_even = slot_even + ((diff >> even[position]) & 1) * (1 << position)
            slot_odd = slot_odd + ((diff >> odd[position]) & 1) * (1 << position)
        return jnp.where(order_parity == 0, slot_even, slot_odd)

    return held, slot_of, parity


def shards(matrix, fill_mask, col_rows, inverses):
    col_index = lax.axis_index("col")
    row_index = lax.axis_index("row")
    row_count = lax.axis_size("row")
    col_count = lax.axis_size("col")
    local_rows, width = matrix.shape
    col_panels = width // PW
    block_rows = local_rows // RB
    local_slabs = local_rows // PW
    mask_f = fill_mask.astype(jnp.bfloat16)

    owner_row = col_rows // local_slabs
    local_ids = row_index * local_slabs + jnp.arange(local_slabs, dtype=jnp.int32)
    choose = jnp.sum((col_rows[None, :] == local_ids[:, None]).astype(jnp.int32), axis=1)
    choose_f = choose.astype(jnp.bfloat16)
    own_slab = jnp.einsum(
        "s,sij->ij",
        choose_f,
        matrix[:, :PW].reshape(local_slabs, PW, PW),
        preferred_element_type=jnp.float32,
    ).astype(jnp.bfloat16)
    slab_mask = jnp.repeat(fill_mask[:, 0], RB // PW).astype(jnp.bfloat16)
    flag_block = jnp.where(
        lax.broadcasted_iota(jnp.int32, (local_slabs, MASK_ROWS, PW), 1) == 0,
        slab_mask[:, None, None],
        jnp.bfloat16(0),
    )
    flag_rows = jnp.einsum(
        "s,sij->ij", choose_f, flag_block, preferred_element_type=jnp.float32
    ).astype(jnp.bfloat16)
    piece = jnp.concatenate((own_slab, flag_rows), axis=0)
    held, slot_of, parity = gather_rows(piece, row_count, col_count)

    mask_rows = jnp.zeros((MASK_ROWS, PW), jnp.bfloat16)
    mask_rows = mask_rows.at[:block_rows].set(jnp.broadcast_to(mask_f[:, 0:1], (block_rows, PW)))
    payload = jnp.concatenate((matrix[:, :PW], mask_rows), axis=0)

    def wanted_of(group):
        own = group * col_panels + jnp.arange(col_panels, dtype=jnp.int32)
        return jnp.concatenate((own, jnp.full((1,), SECOND_COL * col_panels, jnp.int32)))

    def pick(pieces, wanted, order_parity):
        slots = slot_of(owner_row[wanted], order_parity)
        return jnp.take(pieces, slots, axis=0)

    wanted = wanted_of(col_index)
    if col_count == 2:
        swap = [(0, 1), (1, 0)]
        cols_a = payload
        cols_b = lax.ppermute(payload, "col", swap)
        pieces_a = pick(held, wanted, parity)
        for_partner = pick(held, wanted_of(1 - col_index), parity)
        pieces_b = lax.ppermute(for_partner, "col", swap)
    else:
        lead = lax.all_gather(payload, "col", axis=0, tiled=False)
        cols_a, cols_b = lead[FIRST_COL], lead[SECOND_COL]
        everyone = lax.all_gather(held, "col", axis=0, tiled=False)
        pieces_a = pick(everyone[FIRST_COL], wanted, FIRST_COL % 2)
        pieces_b = pick(everyone[SECOND_COL], wanted, SECOND_COL % 2)

    return factor_call(
        matrix, cols_a, cols_b, pieces_a, pieces_b, inverses, fill_mask, col_count == 2
    )


def factor_kernel(
    matrix_ref, cols_a_ref, cols_b_ref, pieces_a_ref, pieces_b_ref, inv_ref, mask_ref, out_ref, *, by_col
):
    local_rows, width = matrix_ref.shape
    col_panels = width // PW
    block_rows = local_rows // RB
    picks = pieces_a_ref.shape[0]
    col_index = lax.axis_index("col")
    swapped = (col_index != FIRST_COL) if by_col else False

    def dot(left, right):
        return jnp.dot(left, right, preferred_element_type=jnp.float32)

    def dot_t(left, right):
        return lax.dot_general(
            left, right, (((1,), (1,)), ((), ())), preferred_element_type=jnp.float32
        )

    def first_second(a_ref, b_ref, index):
        a_val, b_val = a_ref[index], b_ref[index]
        if not by_col:
            return a_val, b_val
        return jnp.where(swapped, b_val, a_val), jnp.where(swapped, a_val, b_val)

    upper = (
        lax.broadcasted_iota(jnp.int32, (PW, PW), 0) <= lax.broadcasted_iota(jnp.int32, (PW, PW), 1)
    )
    zero = jnp.zeros((PW, PW), jnp.bfloat16)
    upper_first = jnp.where(upper, inv_ref[0], zero)
    upper_second = jnp.where(upper, inv_ref[1], zero)

    slabs_first, slabs_second = first_second(
        pieces_a_ref, pieces_b_ref, (slice(None), slice(0, PW), slice(None))
    )
    flags_first, flags_second = first_second(
        pieces_a_ref, pieces_b_ref, (slice(None), slice(PW, PW + 1), slice(None))
    )
    diag_first = (
        dot(slabs_first.reshape(picks * PW, PW), upper_first).reshape(picks, PW, PW)
        * flags_first.astype(jnp.float32)
    ).astype(jnp.bfloat16)
    pivot = diag_first[col_panels]
    own_first = diag_first[:col_panels].reshape(col_panels * PW, PW)
    diag_update = (
        slabs_second[:col_panels].reshape(col_panels * PW, PW).astype(jnp.float32)
        - dot_t(own_first, pivot)
    ).astype(jnp.bfloat16)
    diag_second = (
        dot(diag_update, upper_second).reshape(col_panels, PW, PW)
        * flags_second[:col_panels].astype(jnp.float32)
    ).astype(jnp.bfloat16)

    cols_first, cols_second = first_second(cols_a_ref, cols_b_ref, slice(0, local_rows))
    rows_first, rows_second = first_second(
        cols_a_ref, cols_b_ref, slice(local_rows, local_rows + block_rows)
    )
    first_panel = (
        dot(cols_first, upper_first).reshape(block_rows, RB, PW)
        * rows_first.astype(jnp.float32)[:, None, :]
    ).astype(jnp.bfloat16).reshape(local_rows, PW)
    panel_update = (
        cols_second.astype(jnp.float32) - dot_t(first_panel, pivot)
    ).astype(jnp.bfloat16)
    second_panel = (
        dot(panel_update, upper_second).reshape(block_rows, RB, PW)
        * rows_second.astype(jnp.float32)[:, None, :]
    ).astype(jnp.bfloat16).reshape(local_rows, PW)
    both_panels = jnp.concatenate((first_panel, second_panel), axis=1)

    for j in range(col_panels):
        cols = slice(j * PW, (j + 1) * PW)
        both_diag = jnp.concatenate((diag_first[j], diag_second[j]), axis=1)
        schur = matrix_ref[:, cols].astype(jnp.float32) - dot_t(both_panels, both_diag)
        for b in range(block_rows):
            rows = slice(b * RB, (b + 1) * RB)
            tile = (schur[rows] * mask_ref[b, j].astype(jnp.float32)).astype(jnp.bfloat16)
            if j == 0:
                tile = jnp.where(
                    col_index == FIRST_COL,
                    first_panel[rows],
                    jnp.where(col_index == SECOND_COL, second_panel[rows], tile),
                )
            out_ref[rows, cols] = tile


def factor_call(matrix, cols_a, cols_b, pieces_a, pieces_b, inverses, fill_mask, by_col):
    local_rows, width = matrix.shape
    vmem = pl.BlockSpec(memory_space=pltpu.VMEM)
    smem = pl.BlockSpec(memory_space=pltpu.SMEM)
    flops = 2 * local_rows * width * 2 * PW + 6 * local_rows * PW * PW
    return pl.pallas_call(
        functools.partial(factor_kernel, by_col=by_col),
        out_shape=jax.ShapeDtypeStruct((local_rows, width), jnp.bfloat16),
        in_specs=[vmem] * 6 + [smem],
        out_specs=vmem,
        cost_estimate=pl.CostEstimate(
            flops=flops, bytes_accessed=4 * local_rows * width, transcendentals=0
        ),
    )(matrix, cols_a, cols_b, pieces_a, pieces_b, inverses, fill_mask)


def solution(mesh):
    in_specs = (P("row", "col"), P("row", "col"), P(), P())
    out_specs = P("row", "col")
    return jax.shard_map(shards, mesh=mesh, in_specs=in_specs, out_specs=out_specs, check_vma=False)
```

```python
import functools

import jax
import jax.numpy as jnp
from jax import lax
from jax.experimental import pallas as pl
from jax.experimental.pallas import tpu as pltpu
from jax.sharding import PartitionSpec as P

RB = 256
PW = 128
FIRST_COL = 0
SECOND_COL = 1
MASK_ROWS = 16


def round_orders(bits):
    even = list(range(bits))[::-1]
    odd = list(even)
    for position in range(0, bits - 1, 2):
        odd[position], odd[position + 1] = odd[position + 1], odd[position]
    return even, odd


def gather_rows(piece, row_count, col_count):
    me = lax.axis_index("row")
    parity = lax.axis_index("col") % 2
    bits = row_count.bit_length() - 1
    even, odd = round_orders(bits)
    def exchange(value, masks):
        perm = []
        for r in range(row_count):
            for k in range(col_count):
                perm.append((r * col_count + k, (r ^ masks[k % 2]) * col_count + k))
        return lax.ppermute(value, ("row", "col"), perm)

    held = piece[None]
    first = 0
    if bits >= 2:
        parts = [held]
        for chosen in ((0,), (1,), (0, 1)):
            masks = [sum(1 << order[p] for p in chosen) for order in (even, odd)]
            parts.append(exchange(held, masks))
        held = jnp.concatenate(parts, axis=0)
        first = 2
    for step in range(first, bits):
        masks = [1 << order[step] for order in (even, odd)]
        held = jnp.concatenate((held, exchange(held, masks)), axis=0)

    def slot_of(owner, order_parity):
        diff = jnp.bitwise_xor(owner, me)
        slot_even = jnp.zeros_like(diff)
        slot_odd = jnp.zeros_like(diff)
        for position in range(bits):
            slot_even = slot_even + ((diff >> even[position]) & 1) * (1 << position)
            slot_odd = slot_odd + ((diff >> odd[position]) & 1) * (1 << position)
        return jnp.where(order_parity == 0, slot_even, slot_odd)

    return held, slot_of, parity


def shards(matrix, fill_mask, col_rows, inverses):
    col_index = lax.axis_index("col")
    row_index = lax.axis_index("row")
    row_count = lax.axis_size("row")
    col_count = lax.axis_size("col")
    local_rows, width = matrix.shape
    col_panels = width // PW
    block_rows = local_rows // RB
    local_slabs = local_rows // PW
    mask_f = fill_mask.astype(jnp.bfloat16)

    owner_row = col_rows // local_slabs
    local_ids = row_index * local_slabs + jnp.arange(local_slabs, dtype=jnp.int32)
    choose = jnp.sum((col_rows[None, :] == local_ids[:, None]).astype(jnp.int32), axis=1)
    choose_f = choose.astype(jnp.bfloat16)
    own_slab = jnp.einsum(
        "s,sij->ij",
        choose_f,
        matrix[:, :PW].reshape(local_slabs, PW, PW),
        preferred_element_type=jnp.float32,
    ).astype(jnp.bfloat16)
    slab_mask = jnp.repeat(fill_mask[:, 0], RB // PW).astype(jnp.bfloat16)
    flag_block = jnp.where(
        lax.broadcasted_iota(jnp.int32, (local_slabs, MASK_ROWS, PW), 1) == 0,
        slab_mask[:, None, None],
        jnp.bfloat16(0),
    )
    flag_rows = jnp.einsum(
        "s,sij->ij", choose_f, flag_block, preferred_element_type=jnp.float32
    ).astype(jnp.bfloat16)
    piece = jnp.concatenate((own_slab, flag_rows), axis=0)
    held, slot_of, parity = gather_rows(piece, row_count, col_count)

    mask_rows = jnp.zeros((MASK_ROWS, PW), jnp.bfloat16)
    mask_rows = mask_rows.at[:block_rows].set(jnp.broadcast_to(mask_f[:, 0:1], (block_rows, PW)))
    payload = jnp.concatenate((matrix[:, :PW], mask_rows), axis=0)

    def wanted_of(group):
        own = group * col_panels + jnp.arange(col_panels, dtype=jnp.int32)
        return jnp.concatenate((own, jnp.full((1,), SECOND_COL * col_panels, jnp.int32)))

    def pick(pieces, wanted, order_parity):
        slots = slot_of(owner_row[wanted], order_parity)
        return jnp.take(pieces, slots, axis=0)

    wanted = wanted_of(col_index)
    if col_count == 2:
        swap = [(0, 1), (1, 0)]
        cols_a = payload
        cols_b = lax.ppermute(payload, "col", swap)
        pieces_a = pick(held, wanted, parity)
        for_partner = pick(held, wanted_of(1 - col_index), parity)
        pieces_b = lax.ppermute(for_partner, "col", swap)
    else:
        lead = lax.all_gather(payload, "col", axis=0, tiled=False)
        cols_a, cols_b = lead[FIRST_COL], lead[SECOND_COL]
        everyone = lax.all_gather(held, "col", axis=0, tiled=False)
        pieces_a = pick(everyone[FIRST_COL], wanted, FIRST_COL % 2)
        pieces_b = pick(everyone[SECOND_COL], wanted, SECOND_COL % 2)

    return factor_call(
        matrix, cols_a, cols_b, pieces_a, pieces_b, inverses, fill_mask, col_count == 2
    )


def factor_kernel(
    matrix_ref, cols_a_ref, cols_b_ref, pieces_a_ref, pieces_b_ref, inv_ref, mask_ref, out_ref, *, by_col
):
    local_rows, width = matrix_ref.shape
    col_panels = width // PW
    block_rows = local_rows // RB
    picks = pieces_a_ref.shape[0]
    col_index = lax.axis_index("col")
    swapped = (col_index != FIRST_COL) if by_col else False

    def dot(left, right):
        return jnp.dot(left, right, preferred_element_type=jnp.float32)

    def dot_t(left, right):
        return lax.dot_general(
            left, right, (((1,), (1,)), ((), ())), preferred_element_type=jnp.float32
        )

    def first_second(a_ref, b_ref, index):
        a_val, b_val = a_ref[index], b_ref[index]
        if not by_col:
            return a_val, b_val
        return jnp.where(swapped, b_val, a_val), jnp.where(swapped, a_val, b_val)

    upper = (
        lax.broadcasted_iota(jnp.int32, (PW, PW), 0) <= lax.broadcasted_iota(jnp.int32, (PW, PW), 1)
    )
    zero = jnp.zeros((PW, PW), jnp.bfloat16)
    upper_first = jnp.where(upper, inv_ref[0], zero)
    upper_second = jnp.where(upper, inv_ref[1], zero)

    slabs_first, slabs_second = first_second(
        pieces_a_ref, pieces_b_ref, (slice(None), slice(0, PW), slice(None))
    )
    flags_first, flags_second = first_second(
        pieces_a_ref, pieces_b_ref, (slice(None), slice(PW, PW + 1), slice(None))
    )
    diag_first = (
        dot(slabs_first.reshape(picks * PW, PW), upper_first).reshape(picks, PW, PW)
        * flags_first.astype(jnp.float32)
    ).astype(jnp.bfloat16)
    pivot = diag_first[col_panels]
    own_first = diag_first[:col_panels].reshape(col_panels * PW, PW)
    diag_update = (
        slabs_second[:col_panels].reshape(col_panels * PW, PW).astype(jnp.float32)
        - dot_t(own_first, pivot)
    ).astype(jnp.bfloat16)
    diag_second = (
        dot(diag_update, upper_second).reshape(col_panels, PW, PW)
        * flags_second[:col_panels].astype(jnp.float32)
    ).astype(jnp.bfloat16)

    cols_first, cols_second = first_second(cols_a_ref, cols_b_ref, slice(0, local_rows))
    rows_first, rows_second = first_second(
        cols_a_ref, cols_b_ref, slice(local_rows, local_rows + block_rows)
    )
    first_panel = (
        dot(cols_first, upper_first).reshape(block_rows, RB, PW)
        * rows_first.astype(jnp.float32)[:, None, :]
    ).astype(jnp.bfloat16).reshape(local_rows, PW)
    panel_update = (
        cols_second.astype(jnp.float32) - dot_t(first_panel, pivot)
    ).astype(jnp.bfloat16)
    second_panel = (
        dot(panel_update, upper_second).reshape(block_rows, RB, PW)
        * rows_second.astype(jnp.float32)[:, None, :]
    ).astype(jnp.bfloat16).reshape(local_rows, PW)
    both_panels = jnp.concatenate((first_panel, second_panel), axis=1)

    for j in range(col_panels):
        cols = slice(j * PW, (j + 1) * PW)
        both_diag = jnp.concatenate((diag_first[j], diag_second[j]), axis=1)
        schur = matrix_ref[:, cols].astype(jnp.float32) - dot_t(both_panels, both_diag)
        for b in range(block_rows):
            rows = slice(b * RB, (b + 1) * RB)
            tile = (schur[rows] * mask_ref[b, j].astype(jnp.float32)).astype(jnp.bfloat16)
            if j == 0:
                tile = jnp.where(
                    col_index == FIRST_COL,
                    first_panel[rows],
                    jnp.where(col_index == SECOND_COL, second_panel[rows], tile),
                )
            out_ref[rows, cols] = tile


def factor_call(matrix, cols_a, cols_b, pieces_a, pieces_b, inverses, fill_mask, by_col):
    local_rows, width = matrix.shape
    vmem = pl.BlockSpec(memory_space=pltpu.VMEM)
    smem = pl.BlockSpec(memory_space=pltpu.SMEM)
    flops = 2 * local_rows * width * 2 * PW + 6 * local_rows * PW * PW
    return pl.pallas_call(
        functools.partial(factor_kernel, by_col=by_col),
        out_shape=jax.ShapeDtypeStruct((local_rows, width), jnp.bfloat16),
        in_specs=[vmem] * 6 + [smem],
        out_specs=vmem,
        cost_estimate=pl.CostEstimate(
            flops=flops, bytes_accessed=4 * local_rows * width, transcendentals=0
        ),
    )(matrix, cols_a, cols_b, pieces_a, pieces_b, inverses, fill_mask)


def solution(mesh):
    in_specs = (P("row", "col"), P("row", "col"), P(), P())
    out_specs = P("row", "col")
    return jax.shard_map(shards, mesh=mesh, in_specs=in_specs, out_specs=out_specs, check_vma=False)
```

```python
import functools

import jax
import jax.numpy as jnp
from jax import lax
from jax.experimental import pallas as pl
from jax.experimental.pallas import tpu as pltpu
from jax.sharding import PartitionSpec as P

RB = 256
PW = 128
FIRST_COL = 0
SECOND_COL = 1
MASK_ROWS = 16


def round_orders(bits):
    even = list(range(bits))[::-1]
    odd = list(even)
    for position in range(0, bits - 1, 2):
        odd[position], odd[position + 1] = odd[position + 1], odd[position]
    return even, odd


def gather_rows(piece, row_count, col_count):
    me = lax.axis_index("row")
    parity = lax.axis_index("col") % 2
    bits = row_count.bit_length() - 1
    even, odd = round_orders(bits)
    def exchange(value, masks):
        perm = []
        for r in range(row_count):
            for k in range(col_count):
                perm.append((r * col_count + k, (r ^ masks[k % 2]) * col_count + k))
        return lax.ppermute(value, ("row", "col"), perm)

    held = piece[None]
    for start in range(0, bits, 2):
        groups = ((start,), (start + 1,), (start, start + 1)) if start + 1 < bits else ((start,),)
        parts = [held]
        for chosen in groups:
            masks = [sum(1 << order[p] for p in chosen) for order in (even, odd)]
            parts.append(exchange(held, masks))
        held = jnp.concatenate(parts, axis=0)

    def slot_of(owner, order_parity):
        diff = jnp.bitwise_xor(owner, me)
        slot_even = jnp.zeros_like(diff)
        slot_odd = jnp.zeros_like(diff)
        for position in range(bits):
            slot_even = slot_even + ((diff >> even[position]) & 1) * (1 << position)
            slot_odd = slot_odd + ((diff >> odd[position]) & 1) * (1 << position)
        return jnp.where(order_parity == 0, slot_even, slot_odd)

    return held, slot_of, parity


def shards(matrix, fill_mask, col_rows, inverses):
    col_index = lax.axis_index("col")
    row_index = lax.axis_index("row")
    row_count = lax.axis_size("row")
    col_count = lax.axis_size("col")
    local_rows, width = matrix.shape
    col_panels = width // PW
    block_rows = local_rows // RB
    local_slabs = local_rows // PW
    mask_f = fill_mask.astype(jnp.bfloat16)

    owner_row = col_rows // local_slabs
    local_ids = row_index * local_slabs + jnp.arange(local_slabs, dtype=jnp.int32)
    choose = jnp.sum((col_rows[None, :] == local_ids[:, None]).astype(jnp.int32), axis=1)
    choose_f = choose.astype(jnp.bfloat16)
    own_slab = jnp.einsum(
        "s,sij->ij",
        choose_f,
        matrix[:, :PW].reshape(local_slabs, PW, PW),
        preferred_element_type=jnp.float32,
    ).astype(jnp.bfloat16)
    slab_mask = jnp.repeat(fill_mask[:, 0], RB // PW).astype(jnp.bfloat16)
    flag_block = jnp.where(
        lax.broadcasted_iota(jnp.int32, (local_slabs, MASK_ROWS, PW), 1) == 0,
        slab_mask[:, None, None],
        jnp.bfloat16(0),
    )
    flag_rows = jnp.einsum(
        "s,sij->ij", choose_f, flag_block, preferred_element_type=jnp.float32
    ).astype(jnp.bfloat16)
    piece = jnp.concatenate((own_slab, flag_rows), axis=0)
    held, slot_of, parity = gather_rows(piece, row_count, col_count)

    mask_rows = jnp.zeros((MASK_ROWS, PW), jnp.bfloat16)
    mask_rows = mask_rows.at[:block_rows].set(jnp.broadcast_to(mask_f[:, 0:1], (block_rows, PW)))
    payload = jnp.concatenate((matrix[:, :PW], mask_rows), axis=0)

    def wanted_of(group):
        own = group * col_panels + jnp.arange(col_panels, dtype=jnp.int32)
        return jnp.concatenate((own, jnp.full((1,), SECOND_COL * col_panels, jnp.int32)))

    def pick(pieces, wanted, order_parity):
        slots = slot_of(owner_row[wanted], order_parity)
        return jnp.take(pieces, slots, axis=0)

    wanted = wanted_of(col_index)
    if col_count == 2:
        swap = [(0, 1), (1, 0)]
        cols_a = payload
        cols_b = lax.ppermute(payload, "col", swap)
        pieces_a = pick(held, wanted, parity)
        for_partner = pick(held, wanted_of(1 - col_index), parity)
        pieces_b = lax.ppermute(for_partner, "col", swap)
    else:
        lead = lax.all_gather(payload, "col", axis=0, tiled=False)
        cols_a, cols_b = lead[FIRST_COL], lead[SECOND_COL]
        everyone = lax.all_gather(held, "col", axis=0, tiled=False)
        pieces_a = pick(everyone[FIRST_COL], wanted, FIRST_COL % 2)
        pieces_b = pick(everyone[SECOND_COL], wanted, SECOND_COL % 2)

    return factor_call(
        matrix, cols_a, cols_b, pieces_a, pieces_b, inverses, fill_mask, col_count == 2
    )


def factor_kernel(
    matrix_ref, cols_a_ref, cols_b_ref, pieces_a_ref, pieces_b_ref, inv_ref, mask_ref, out_ref, *, by_col
):
    local_rows, width = matrix_ref.shape
    col_panels = width // PW
    block_rows = local_rows // RB
    picks = pieces_a_ref.shape[0]
    col_index = lax.axis_index("col")
    swapped = (col_index != FIRST_COL) if by_col else False

    def dot(left, right):
        return jnp.dot(left, right, preferred_element_type=jnp.float32)

    def dot_t(left, right):
        return lax.dot_general(
            left, right, (((1,), (1,)), ((), ())), preferred_element_type=jnp.float32
        )

    def first_second(a_ref, b_ref, index):
        a_val, b_val = a_ref[index], b_ref[index]
        if not by_col:
            return a_val, b_val
        return jnp.where(swapped, b_val, a_val), jnp.where(swapped, a_val, b_val)

    upper = (
        lax.broadcasted_iota(jnp.int32, (PW, PW), 0) <= lax.broadcasted_iota(jnp.int32, (PW, PW), 1)
    )
    zero = jnp.zeros((PW, PW), jnp.bfloat16)
    upper_first = jnp.where(upper, inv_ref[0], zero)
    upper_second = jnp.where(upper, inv_ref[1], zero)

    slabs_first, slabs_second = first_second(
        pieces_a_ref, pieces_b_ref, (slice(None), slice(0, PW), slice(None))
    )
    flags_first, flags_second = first_second(
        pieces_a_ref, pieces_b_ref, (slice(None), slice(PW, PW + 1), slice(None))
    )
    diag_first = (
        dot(slabs_first.reshape(picks * PW, PW), upper_first).reshape(picks, PW, PW)
        * flags_first.astype(jnp.float32)
    ).astype(jnp.bfloat16)
    pivot = diag_first[col_panels]
    own_first = diag_first[:col_panels].reshape(col_panels * PW, PW)
    diag_update = (
        slabs_second[:col_panels].reshape(col_panels * PW, PW).astype(jnp.float32)
        - dot_t(own_first, pivot)
    ).astype(jnp.bfloat16)
    diag_second = (
        dot(diag_update, upper_second).reshape(col_panels, PW, PW)
        * flags_second[:col_panels].astype(jnp.float32)
    ).astype(jnp.bfloat16)

    cols_first, cols_second = first_second(cols_a_ref, cols_b_ref, slice(0, local_rows))
    rows_first, rows_second = first_second(
        cols_a_ref, cols_b_ref, slice(local_rows, local_rows + block_rows)
    )
    first_panel = (
        dot(cols_first, upper_first).reshape(block_rows, RB, PW)
        * rows_first.astype(jnp.float32)[:, None, :]
    ).astype(jnp.bfloat16).reshape(local_rows, PW)
    panel_update = (
        cols_second.astype(jnp.float32) - dot_t(first_panel, pivot)
    ).astype(jnp.bfloat16)
    second_panel = (
        dot(panel_update, upper_second).reshape(block_rows, RB, PW)
        * rows_second.astype(jnp.float32)[:, None, :]
    ).astype(jnp.bfloat16).reshape(local_rows, PW)
    both_panels = jnp.concatenate((first_panel, second_panel), axis=1)

    for j in range(col_panels):
        cols = slice(j * PW, (j + 1) * PW)
        both_diag = jnp.concatenate((diag_first[j], diag_second[j]), axis=1)
        schur = matrix_ref[:, cols].astype(jnp.float32) - dot_t(both_panels, both_diag)
        for b in range(block_rows):
            rows = slice(b * RB, (b + 1) * RB)
            tile = (schur[rows] * mask_ref[b, j].astype(jnp.float32)).astype(jnp.bfloat16)
            if j == 0:
                tile = jnp.where(
                    col_index == FIRST_COL,
                    first_panel[rows],
                    jnp.where(col_index == SECOND_COL, second_panel[rows], tile),
                )
            out_ref[rows, cols] = tile


def factor_call(matrix, cols_a, cols_b, pieces_a, pieces_b, inverses, fill_mask, by_col):
    local_rows, width = matrix.shape
    vmem = pl.BlockSpec(memory_space=pltpu.VMEM)
    smem = pl.BlockSpec(memory_space=pltpu.SMEM)
    flops = 2 * local_rows * width * 2 * PW + 6 * local_rows * PW * PW
    return pl.pallas_call(
        functools.partial(factor_kernel, by_col=by_col),
        out_shape=jax.ShapeDtypeStruct((local_rows, width), jnp.bfloat16),
        in_specs=[vmem] * 6 + [smem],
        out_specs=vmem,
        cost_estimate=pl.CostEstimate(
            flops=flops, bytes_accessed=4 * local_rows * width, transcendentals=0
        ),
    )(matrix, cols_a, cols_b, pieces_a, pieces_b, inverses, fill_mask)


def solution(mesh):
    in_specs = (P("row", "col"), P("row", "col"), P(), P())
    out_specs = P("row", "col")
    return jax.shard_map(shards, mesh=mesh, in_specs=in_specs, out_specs=out_specs, check_vma=False)
```

```python
import functools

import jax
import jax.numpy as jnp
from jax import lax
from jax.experimental import pallas as pl
from jax.experimental.pallas import tpu as pltpu
from jax.sharding import PartitionSpec as P

RB = 256
PW = 128
FIRST_COL = 0
SECOND_COL = 1
MASK_ROWS = 16


def round_orders(bits):
    even = list(range(bits))[::-1]
    odd = list(even)
    for position in range(0, bits - 1, 2):
        odd[position], odd[position + 1] = odd[position + 1], odd[position]
    return even, odd


def gather_rows(piece, row_count, col_count):
    me = lax.axis_index("row")
    parity = lax.axis_index("col") % 2
    bits = row_count.bit_length() - 1
    even, odd = round_orders(bits)
    def exchange(value, masks):
        perm = []
        for r in range(row_count):
            for k in range(col_count):
                perm.append((r * col_count + k, (r ^ masks[k % 2]) * col_count + k))
        return lax.ppermute(value, ("row", "col"), perm)

    held = piece[None]
    for start in range(0, bits, 2):
        groups = ((start,), (start + 1,), (start, start + 1)) if start + 1 < bits else ((start,),)
        parts = [held]
        for chosen in groups:
            masks = [sum(1 << order[p] for p in chosen) for order in (even, odd)]
            parts.append(exchange(held, masks))
        held = jnp.concatenate(parts, axis=0)

    def slot_of(owner, order_parity):
        diff = jnp.bitwise_xor(owner, me)
        slot_even = jnp.zeros_like(diff)
        slot_odd = jnp.zeros_like(diff)
        for position in range(bits):
            slot_even = slot_even + ((diff >> even[position]) & 1) * (1 << position)
            slot_odd = slot_odd + ((diff >> odd[position]) & 1) * (1 << position)
        return jnp.where(order_parity == 0, slot_even, slot_odd)

    return held, slot_of, parity


def shards(matrix, fill_mask, col_rows, inverses):
    col_index = lax.axis_index("col")
    row_index = lax.axis_index("row")
    row_count = lax.axis_size("row")
    col_count = lax.axis_size("col")
    local_rows, width = matrix.shape
    col_panels = width // PW
    block_rows = local_rows // RB
    local_slabs = local_rows // PW
    mask_f = fill_mask.astype(jnp.bfloat16)

    owner_row = col_rows // local_slabs
    local_ids = row_index * local_slabs + jnp.arange(local_slabs, dtype=jnp.int32)
    choose = jnp.sum((col_rows[None, :] == local_ids[:, None]).astype(jnp.int32), axis=1)
    choose_f = choose.astype(jnp.bfloat16)
    own_slab = jnp.einsum(
        "s,sij->ij",
        choose_f,
        matrix[:, :PW].reshape(local_slabs, PW, PW),
        preferred_element_type=jnp.float32,
    ).astype(jnp.bfloat16)
    slab_mask = jnp.repeat(fill_mask[:, 0], RB // PW).astype(jnp.bfloat16)
    flag_block = jnp.where(
        lax.broadcasted_iota(jnp.int32, (local_slabs, MASK_ROWS, PW), 1) == 0,
        slab_mask[:, None, None],
        jnp.bfloat16(0),
    )
    flag_rows = jnp.einsum(
        "s,sij->ij", choose_f, flag_block, preferred_element_type=jnp.float32
    ).astype(jnp.bfloat16)
    piece = jnp.concatenate((own_slab, flag_rows), axis=0)
    held, slot_of, parity = gather_rows(piece, row_count, col_count)

    mask_rows = jnp.zeros((MASK_ROWS, PW), jnp.bfloat16)
    mask_rows = mask_rows.at[:block_rows].set(jnp.broadcast_to(mask_f[:, 0:1], (block_rows, PW)))
    payload = jnp.concatenate((matrix[:, :PW], mask_rows), axis=0)

    def wanted_of(group):
        own = group * col_panels + jnp.arange(col_panels, dtype=jnp.int32)
        return jnp.concatenate((own, jnp.full((1,), SECOND_COL * col_panels, jnp.int32)))

    def pick(pieces, wanted, order_parity):
        slots = slot_of(owner_row[wanted], order_parity)
        return jnp.take(pieces, slots, axis=0)

    wanted = wanted_of(col_index)
    if col_count == 2:
        swap = [(0, 1), (1, 0)]
        cols_a = payload
        cols_b = lax.ppermute(payload, "col", swap)
        pieces_a = pick(held, wanted, parity)
        for_partner = pick(held, wanted_of(1 - col_index), parity)
        pieces_b = lax.ppermute(for_partner, "col", swap)
    else:
        lead = lax.all_gather(payload, "col", axis=0, tiled=False)
        cols_a, cols_b = lead[FIRST_COL], lead[SECOND_COL]
        everyone = lax.all_gather(held, "col", axis=0, tiled=False)
        pieces_a = pick(everyone[FIRST_COL], wanted, FIRST_COL % 2)
        pieces_b = pick(everyone[SECOND_COL], wanted, SECOND_COL % 2)

    return factor_call(
        matrix, cols_a, cols_b, pieces_a, pieces_b, inverses, fill_mask, col_count == 2
    )


def factor_kernel(
    matrix_hbm, cols_a_hbm, cols_b_hbm, pieces_a_hbm, pieces_b_hbm, inv_ref, mask_ref, out_hbm,
    matrix_ref, cols_a_ref, cols_b_ref, pieces_a_ref, pieces_b_ref, out_ref, in_sems, matrix_sems, out_sems,
    *, by_col
):
    local_rows, width = matrix_ref.shape
    col_panels = width // PW
    block_rows = local_rows // RB
    picks = pieces_a_ref.shape[0]
    small = [
        pltpu.make_async_copy(src, dst, in_sems.at[i])
        for i, (src, dst) in enumerate(
            (
                (pieces_a_hbm, pieces_a_ref),
                (pieces_b_hbm, pieces_b_ref),
                (cols_a_hbm, cols_a_ref),
                (cols_b_hbm, cols_b_ref),
            )
        )
    ]
    for copy in small:
        copy.start()
    matrix_in = []
    for b in range(block_rows):
        rows = pl.ds(b * RB, RB)
        copy = pltpu.make_async_copy(matrix_hbm.at[rows], matrix_ref.at[rows], matrix_sems.at[b])
        copy.start()
        matrix_in.append(copy)
    small[0].wait()
    small[1].wait()
    col_index = lax.axis_index("col")
    swapped = (col_index != FIRST_COL) if by_col else False

    def dot(left, right):
        return jnp.dot(left, right, preferred_element_type=jnp.float32)

    def dot_t(left, right):
        return lax.dot_general(
            left, right, (((1,), (1,)), ((), ())), preferred_element_type=jnp.float32
        )

    def first_second(a_ref, b_ref, index):
        a_val, b_val = a_ref[index], b_ref[index]
        if not by_col:
            return a_val, b_val
        return jnp.where(swapped, b_val, a_val), jnp.where(swapped, a_val, b_val)

    upper = (
        lax.broadcasted_iota(jnp.int32, (PW, PW), 0) <= lax.broadcasted_iota(jnp.int32, (PW, PW), 1)
    )
    zero = jnp.zeros((PW, PW), jnp.bfloat16)
    upper_first = jnp.where(upper, inv_ref[0], zero)
    upper_second = jnp.where(upper, inv_ref[1], zero)

    slabs_first, slabs_second = first_second(
        pieces_a_ref, pieces_b_ref, (slice(None), slice(0, PW), slice(None))
    )
    flags_first, flags_second = first_second(
        pieces_a_ref, pieces_b_ref, (slice(None), slice(PW, PW + 1), slice(None))
    )
    diag_first = (
        dot(slabs_first.reshape(picks * PW, PW), upper_first).reshape(picks, PW, PW)
        * flags_first.astype(jnp.float32)
    ).astype(jnp.bfloat16)
    pivot = diag_first[col_panels]
    own_first = diag_first[:col_panels].reshape(col_panels * PW, PW)
    diag_update = (
        slabs_second[:col_panels].reshape(col_panels * PW, PW).astype(jnp.float32)
        - dot_t(own_first, pivot)
    ).astype(jnp.bfloat16)
    diag_second = (
        dot(diag_update, upper_second).reshape(col_panels, PW, PW)
        * flags_second[:col_panels].astype(jnp.float32)
    ).astype(jnp.bfloat16)

    small[2].wait()
    small[3].wait()
    cols_first, cols_second = first_second(cols_a_ref, cols_b_ref, slice(0, local_rows))
    rows_first, rows_second = first_second(
        cols_a_ref, cols_b_ref, slice(local_rows, local_rows + block_rows)
    )
    first_panel = (
        dot(cols_first, upper_first).reshape(block_rows, RB, PW)
        * rows_first.astype(jnp.float32)[:, None, :]
    ).astype(jnp.bfloat16).reshape(local_rows, PW)
    panel_update = (
        cols_second.astype(jnp.float32) - dot_t(first_panel, pivot)
    ).astype(jnp.bfloat16)
    second_panel = (
        dot(panel_update, upper_second).reshape(block_rows, RB, PW)
        * rows_second.astype(jnp.float32)[:, None, :]
    ).astype(jnp.bfloat16).reshape(local_rows, PW)
    both_panels = jnp.concatenate((first_panel, second_panel), axis=1)

    both_diag = [
        jnp.concatenate((diag_first[j], diag_second[j]), axis=1) for j in range(col_panels)
    ]
    matrix_out = []
    for b in range(block_rows):
        rows = slice(b * RB, (b + 1) * RB)
        matrix_in[b].wait()
        panels_rows = both_panels[rows]
        for j in range(col_panels):
            cols = slice(j * PW, (j + 1) * PW)
            schur = matrix_ref[rows, cols].astype(jnp.float32) - dot_t(panels_rows, both_diag[j])
            tile = (schur * mask_ref[b, j].astype(jnp.float32)).astype(jnp.bfloat16)
            if j == 0:
                tile = jnp.where(
                    col_index == FIRST_COL,
                    first_panel[rows],
                    jnp.where(col_index == SECOND_COL, second_panel[rows], tile),
                )
            out_ref[rows, cols] = tile
        copy = pltpu.make_async_copy(
            out_ref.at[pl.ds(b * RB, RB)], out_hbm.at[pl.ds(b * RB, RB)], out_sems.at[b]
        )
        copy.start()
        matrix_out.append(copy)
    for copy in matrix_out:
        copy.wait()


def factor_call(matrix, cols_a, cols_b, pieces_a, pieces_b, inverses, fill_mask, by_col):
    local_rows, width = matrix.shape
    vmem = pl.BlockSpec(memory_space=pltpu.VMEM)
    smem = pl.BlockSpec(memory_space=pltpu.SMEM)
    hbm = pl.BlockSpec(memory_space=pl.ANY)
    flops = 2 * local_rows * width * 2 * PW + 6 * local_rows * PW * PW
    return pl.pallas_call(
        functools.partial(factor_kernel, by_col=by_col),
        out_shape=jax.ShapeDtypeStruct((local_rows, width), jnp.bfloat16),
        in_specs=[hbm] * 5 + [vmem, smem],
        out_specs=hbm,
        scratch_shapes=[
            pltpu.VMEM((local_rows, width), jnp.bfloat16),
            pltpu.VMEM(cols_a.shape, jnp.bfloat16),
            pltpu.VMEM(cols_b.shape, jnp.bfloat16),
            pltpu.VMEM(pieces_a.shape, jnp.bfloat16),
            pltpu.VMEM(pieces_b.shape, jnp.bfloat16),
            pltpu.VMEM((local_rows, width), jnp.bfloat16),
            pltpu.SemaphoreType.DMA((4,)),
            pltpu.SemaphoreType.DMA((local_rows // RB,)),
            pltpu.SemaphoreType.DMA((local_rows // RB,)),
        ],
        cost_estimate=pl.CostEstimate(
            flops=flops, bytes_accessed=4 * local_rows * width, transcendentals=0
        ),
    )(matrix, cols_a, cols_b, pieces_a, pieces_b, inverses, fill_mask)


def solution(mesh):
    in_specs = (P("row", "col"), P("row", "col"), P(), P())
    out_specs = P("row", "col")
    return jax.shard_map(shards, mesh=mesh, in_specs=in_specs, out_specs=out_specs, check_vma=False)
```

```python
import functools

import jax
import jax.numpy as jnp
from jax import lax
from jax.experimental import pallas as pl
from jax.experimental.pallas import tpu as pltpu
from jax.sharding import PartitionSpec as P

RB = 256
PW = 128
FIRST_COL = 0
SECOND_COL = 1
MASK_ROWS = 16


def round_orders(bits):
    even = list(range(bits))[::-1]
    odd = list(even)
    for position in range(0, bits - 1, 2):
        odd[position], odd[position + 1] = odd[position + 1], odd[position]
    return even, odd


def gather_rows(piece, row_count, col_count):
    me = lax.axis_index("row")
    parity = lax.axis_index("col") % 2
    bits = row_count.bit_length() - 1
    even, odd = round_orders(bits)
    def exchange(value, masks):
        perm = []
        for r in range(row_count):
            for k in range(col_count):
                perm.append((r * col_count + k, (r ^ masks[k % 2]) * col_count + k))
        return lax.ppermute(value, ("row", "col"), perm)

    held = piece[None]
    for start in range(0, bits, 2):
        groups = ((start,), (start + 1,), (start, start + 1)) if start + 1 < bits else ((start,),)
        parts = [held]
        for chosen in groups:
            masks = [sum(1 << order[p] for p in chosen) for order in (even, odd)]
            parts.append(exchange(held, masks))
        held = jnp.concatenate(parts, axis=0)

    def slot_of(owner, order_parity):
        diff = jnp.bitwise_xor(owner, me)
        slot_even = jnp.zeros_like(diff)
        slot_odd = jnp.zeros_like(diff)
        for position in range(bits):
            slot_even = slot_even + ((diff >> even[position]) & 1) * (1 << position)
            slot_odd = slot_odd + ((diff >> odd[position]) & 1) * (1 << position)
        return jnp.where(order_parity == 0, slot_even, slot_odd)

    return held, slot_of, parity


def shards(matrix, fill_mask, col_rows, inverses):
    col_index = lax.axis_index("col")
    row_index = lax.axis_index("row")
    row_count = lax.axis_size("row")
    col_count = lax.axis_size("col")
    local_rows, width = matrix.shape
    col_panels = width // PW
    block_rows = local_rows // RB
    local_slabs = local_rows // PW

    owner_row = col_rows // local_slabs
    piece, payload = prep_call(matrix, col_rows, fill_mask)
    held, slot_of, parity = gather_rows(piece, row_count, col_count)

    def wanted_of(group):
        own = group * col_panels + jnp.arange(col_panels, dtype=jnp.int32)
        return jnp.concatenate((own, jnp.full((1,), SECOND_COL * col_panels, jnp.int32)))

    def pick(pieces, wanted, order_parity):
        slots = slot_of(owner_row[wanted], order_parity)
        return jnp.take(pieces, slots, axis=0)

    wanted = wanted_of(col_index)
    if col_count == 2:
        swap = [(0, 1), (1, 0)]
        cols_a = payload
        cols_b = lax.ppermute(payload, "col", swap)
        pieces_a = pick(held, wanted, parity)
        for_partner = pick(held, wanted_of(1 - col_index), parity)
        pieces_b = lax.ppermute(for_partner, "col", swap)
    else:
        lead = lax.all_gather(payload, "col", axis=0, tiled=False)
        cols_a, cols_b = lead[FIRST_COL], lead[SECOND_COL]
        everyone = lax.all_gather(held, "col", axis=0, tiled=False)
        pieces_a = pick(everyone[FIRST_COL], wanted, FIRST_COL % 2)
        pieces_b = pick(everyone[SECOND_COL], wanted, SECOND_COL % 2)

    return factor_call(
        matrix, cols_a, cols_b, pieces_a, pieces_b, inverses, fill_mask, col_count == 2
    )


def prep_kernel(lead_ref, col_rows_ref, mask_ref, piece_ref, payload_ref):
    local_rows = lead_ref.shape[0]
    local_slabs = local_rows // PW
    block_rows = local_rows // RB
    row_index = lax.axis_index("row")
    place = jnp.int32(0)
    for c in range(col_rows_ref.shape[0]):
        entry = col_rows_ref[c]
        place = place + jnp.where(entry // local_slabs == row_index, entry % local_slabs, 0)
    place = jnp.minimum(place, local_slabs - 1)
    start = pl.multiple_of(place * PW, PW)
    piece_ref[0:PW, :] = lead_ref[pl.ds(start, PW), :]
    flag = mask_ref[place // (RB // PW), 0].astype(jnp.float32)
    row_ids = lax.broadcasted_iota(jnp.int32, (MASK_ROWS, PW), 0)
    piece_ref[PW : PW + MASK_ROWS, :] = jnp.where(row_ids == 0, flag, 0.0).astype(jnp.bfloat16)
    payload_ref[0:local_rows, :] = lead_ref[...]
    mask_rows = jnp.zeros((MASK_ROWS, PW), jnp.float32)
    for b in range(block_rows):
        mask_rows = jnp.where(row_ids == b, mask_ref[b, 0].astype(jnp.float32), mask_rows)
    payload_ref[local_rows : local_rows + MASK_ROWS, :] = mask_rows.astype(jnp.bfloat16)


def prep_call(matrix, col_rows, fill_mask):
    local_rows = matrix.shape[0]
    smem = pl.BlockSpec(memory_space=pltpu.SMEM)
    return pl.pallas_call(
        prep_kernel,
        out_shape=(
            jax.ShapeDtypeStruct((PW + MASK_ROWS, PW), jnp.bfloat16),
            jax.ShapeDtypeStruct((local_rows + MASK_ROWS, PW), jnp.bfloat16),
        ),
        grid=(1,),
        in_specs=[pl.BlockSpec((local_rows, PW), lambda i: (0, 0)), smem, smem],
        out_specs=(
            pl.BlockSpec((PW + MASK_ROWS, PW), lambda i: (0, 0)),
            pl.BlockSpec((local_rows + MASK_ROWS, PW), lambda i: (0, 0)),
        ),
        cost_estimate=pl.CostEstimate(
            flops=0, bytes_accessed=4 * local_rows * PW, transcendentals=0
        ),
    )(matrix, col_rows, fill_mask)


def factor_kernel(
    matrix_ref, cols_a_ref, cols_b_ref, pieces_a_ref, pieces_b_ref, inv_ref, mask_ref, out_ref, *, by_col
):
    local_rows, width = matrix_ref.shape
    col_panels = width // PW
    block_rows = local_rows // RB
    picks = pieces_a_ref.shape[0]
    col_index = lax.axis_index("col")
    swapped = (col_index != FIRST_COL) if by_col else False

    def dot(left, right):
        return jnp.dot(left, right, preferred_element_type=jnp.float32)

    def dot_t(left, right):
        return lax.dot_general(
            left, right, (((1,), (1,)), ((), ())), preferred_element_type=jnp.float32
        )

    def first_second(a_ref, b_ref, index):
        a_val, b_val = a_ref[index], b_ref[index]
        if not by_col:
            return a_val, b_val
        return jnp.where(swapped, b_val, a_val), jnp.where(swapped, a_val, b_val)

    upper = (
        lax.broadcasted_iota(jnp.int32, (PW, PW), 0) <= lax.broadcasted_iota(jnp.int32, (PW, PW), 1)
    )
    zero = jnp.zeros((PW, PW), jnp.bfloat16)
    upper_first = jnp.where(upper, inv_ref[0], zero)
    upper_second = jnp.where(upper, inv_ref[1], zero)

    slabs_first, slabs_second = first_second(
        pieces_a_ref, pieces_b_ref, (slice(None), slice(0, PW), slice(None))
    )
    flags_first, flags_second = first_second(
        pieces_a_ref, pieces_b_ref, (slice(None), slice(PW, PW + 1), slice(None))
    )
    diag_first = (
        dot(slabs_first.reshape(picks * PW, PW), upper_first).reshape(picks, PW, PW)
        * flags_first.astype(jnp.float32)
    ).astype(jnp.bfloat16)
    pivot = diag_first[col_panels]
    own_first = diag_first[:col_panels].reshape(col_panels * PW, PW)
    diag_update = (
        slabs_second[:col_panels].reshape(col_panels * PW, PW).astype(jnp.float32)
        - dot_t(own_first, pivot)
    ).astype(jnp.bfloat16)
    diag_second = (
        dot(diag_update, upper_second).reshape(col_panels, PW, PW)
        * flags_second[:col_panels].astype(jnp.float32)
    ).astype(jnp.bfloat16)

    cols_first, cols_second = first_second(cols_a_ref, cols_b_ref, slice(0, local_rows))
    rows_first, rows_second = first_second(
        cols_a_ref, cols_b_ref, slice(local_rows, local_rows + block_rows)
    )
    first_panel = (
        dot(cols_first, upper_first).reshape(block_rows, RB, PW)
        * rows_first.astype(jnp.float32)[:, None, :]
    ).astype(jnp.bfloat16).reshape(local_rows, PW)
    panel_update = (
        cols_second.astype(jnp.float32) - dot_t(first_panel, pivot)
    ).astype(jnp.bfloat16)
    second_panel = (
        dot(panel_update, upper_second).reshape(block_rows, RB, PW)
        * rows_second.astype(jnp.float32)[:, None, :]
    ).astype(jnp.bfloat16).reshape(local_rows, PW)
    both_panels = jnp.concatenate((first_panel, second_panel), axis=1)

    for j in range(col_panels):
        cols = slice(j * PW, (j + 1) * PW)
        both_diag = jnp.concatenate((diag_first[j], diag_second[j]), axis=1)
        schur = matrix_ref[:, cols].astype(jnp.float32) - dot_t(both_panels, both_diag)
        for b in range(block_rows):
            rows = slice(b * RB, (b + 1) * RB)
            tile = (schur[rows] * mask_ref[b, j].astype(jnp.float32)).astype(jnp.bfloat16)
            if j == 0:
                tile = jnp.where(
                    col_index == FIRST_COL,
                    first_panel[rows],
                    jnp.where(col_index == SECOND_COL, second_panel[rows], tile),
                )
            out_ref[rows, cols] = tile


def factor_call(matrix, cols_a, cols_b, pieces_a, pieces_b, inverses, fill_mask, by_col):
    local_rows, width = matrix.shape
    vmem = pl.BlockSpec(memory_space=pltpu.VMEM)
    smem = pl.BlockSpec(memory_space=pltpu.SMEM)
    flops = 2 * local_rows * width * 2 * PW + 6 * local_rows * PW * PW
    return pl.pallas_call(
        functools.partial(factor_kernel, by_col=by_col),
        out_shape=jax.ShapeDtypeStruct((local_rows, width), jnp.bfloat16),
        in_specs=[vmem] * 6 + [smem],
        out_specs=vmem,
        cost_estimate=pl.CostEstimate(
            flops=flops, bytes_accessed=4 * local_rows * width, transcendentals=0
        ),
    )(matrix, cols_a, cols_b, pieces_a, pieces_b, inverses, fill_mask)


def solution(mesh):
    in_specs = (P("row", "col"), P("row", "col"), P(), P())
    out_specs = P("row", "col")
    return jax.shard_map(shards, mesh=mesh, in_specs=in_specs, out_specs=out_specs, check_vma=False)
```

```python
import functools

import jax
import jax.numpy as jnp
from jax import lax
from jax.experimental import pallas as pl
from jax.experimental.pallas import tpu as pltpu
from jax.sharding import PartitionSpec as P

RB = 256
PW = 128
FIRST_COL = 0
SECOND_COL = 1
MASK_ROWS = 16


def round_orders(bits):
    even = list(range(bits))[::-1]
    odd = list(even)
    for position in range(0, bits - 1, 2):
        odd[position], odd[position + 1] = odd[position + 1], odd[position]
    return even, odd


def gather_rows(piece, row_count, col_count):
    me = lax.axis_index("row")
    parity = lax.axis_index("col") % 2
    bits = row_count.bit_length() - 1
    even, odd = round_orders(bits)
    def exchange(value, masks):
        perm = []
        for r in range(row_count):
            for k in range(col_count):
                perm.append((r * col_count + k, (r ^ masks[k % 2]) * col_count + k))
        return lax.ppermute(value, ("row", "col"), perm)

    held = piece[None]
    for start in range(0, bits, 2):
        groups = ((start,), (start + 1,), (start, start + 1)) if start + 1 < bits else ((start,),)
        parts = [held]
        for chosen in groups:
            masks = [sum(1 << order[p] for p in chosen) for order in (even, odd)]
            parts.append(exchange(held, masks))
        held = jnp.concatenate(parts, axis=0)

    def slot_of(owner, order_parity):
        diff = jnp.bitwise_xor(owner, me)
        slot_even = jnp.zeros_like(diff)
        slot_odd = jnp.zeros_like(diff)
        for position in range(bits):
            slot_even = slot_even + ((diff >> even[position]) & 1) * (1 << position)
            slot_odd = slot_odd + ((diff >> odd[position]) & 1) * (1 << position)
        return jnp.where(order_parity == 0, slot_even, slot_odd)

    return held, slot_of, parity


def shards(matrix, fill_mask, col_rows, inverses):
    col_index = lax.axis_index("col")
    row_index = lax.axis_index("row")
    row_count = lax.axis_size("row")
    col_count = lax.axis_size("col")
    local_rows, width = matrix.shape
    col_panels = width // PW
    block_rows = local_rows // RB
    local_slabs = local_rows // PW

    owner_row = col_rows // local_slabs
    piece, payload = prep_call(matrix, col_rows, fill_mask)
    held, slot_of, parity = gather_rows(piece, row_count, col_count)

    def wanted_of(group):
        own = group * col_panels + jnp.arange(col_panels, dtype=jnp.int32)
        return jnp.concatenate((own, jnp.full((1,), SECOND_COL * col_panels, jnp.int32)))

    def pick(pieces, wanted, order_parity):
        slots = slot_of(owner_row[wanted], order_parity)
        return jnp.take(pieces, slots, axis=0)

    wanted = wanted_of(col_index)
    if col_count == 2:
        swap = [(0, 1), (1, 0)]
        cols_a = payload
        cols_b = lax.ppermute(payload, "col", swap)
        pieces_a = pick(held, wanted, parity)
        for_partner = pick(held, wanted_of(1 - col_index), parity)
        pieces_b = lax.ppermute(for_partner, "col", swap)
    else:
        lead = lax.all_gather(payload, "col", axis=0, tiled=False)
        cols_a, cols_b = lead[FIRST_COL], lead[SECOND_COL]
        everyone = lax.all_gather(held, "col", axis=0, tiled=False)
        pieces_a = pick(everyone[FIRST_COL], wanted, FIRST_COL % 2)
        pieces_b = pick(everyone[SECOND_COL], wanted, SECOND_COL % 2)

    return factor_call(
        matrix, cols_a, cols_b, pieces_a, pieces_b, inverses, fill_mask, col_count == 2
    )


def prep_kernel(lead_ref, col_rows_ref, mask_ref, piece_ref, payload_ref):
    local_rows = lead_ref.shape[0]
    local_slabs = local_rows // PW
    block_rows = local_rows // RB
    row_index = lax.axis_index("row")
    place = jnp.int32(0)
    for c in range(col_rows_ref.shape[0]):
        entry = col_rows_ref[c]
        place = place + jnp.where(entry // local_slabs == row_index, entry % local_slabs, 0)
    place = jnp.minimum(place, local_slabs - 1)
    start = pl.multiple_of(place * PW, PW)
    piece_ref[0:PW, :] = lead_ref[pl.ds(start, PW), :]
    flag = mask_ref[place // (RB // PW), 0].astype(jnp.float32)
    row_ids = lax.broadcasted_iota(jnp.int32, (MASK_ROWS, PW), 0)
    piece_ref[PW : PW + MASK_ROWS, :] = jnp.where(row_ids == 0, flag, 0.0).astype(jnp.bfloat16)
    payload_ref[0:local_rows, :] = lead_ref[...]
    mask_rows = jnp.zeros((MASK_ROWS, PW), jnp.float32)
    for b in range(block_rows):
        mask_rows = jnp.where(row_ids == b, mask_ref[b, 0].astype(jnp.float32), mask_rows)
    payload_ref[local_rows : local_rows + MASK_ROWS, :] = mask_rows.astype(jnp.bfloat16)


def prep_call(matrix, col_rows, fill_mask):
    local_rows = matrix.shape[0]
    smem = pl.BlockSpec(memory_space=pltpu.SMEM)
    return pl.pallas_call(
        prep_kernel,
        out_shape=(
            jax.ShapeDtypeStruct((PW + MASK_ROWS, PW), jnp.bfloat16),
            jax.ShapeDtypeStruct((local_rows + MASK_ROWS, PW), jnp.bfloat16),
        ),
        grid=(1,),
        in_specs=[pl.BlockSpec((local_rows, PW), lambda i: (0, 0)), smem, smem],
        out_specs=(
            pl.BlockSpec((PW + MASK_ROWS, PW), lambda i: (0, 0)),
            pl.BlockSpec((local_rows + MASK_ROWS, PW), lambda i: (0, 0)),
        ),
        cost_estimate=pl.CostEstimate(
            flops=0, bytes_accessed=4 * local_rows * PW, transcendentals=0
        ),
    )(matrix, col_rows, fill_mask)


def factor_kernel(
    matrix_hbm, cols_a_ref, cols_b_ref, pieces_a_ref, pieces_b_ref, inv_ref, mask_ref, out_hbm,
    matrix_ref, out_ref, sems, *, by_col
):
    local_rows, width = matrix_ref.shape
    matrix_in = pltpu.make_async_copy(matrix_hbm, matrix_ref, sems.at[0])
    matrix_in.start()
    col_panels = width // PW
    block_rows = local_rows // RB
    picks = pieces_a_ref.shape[0]
    col_index = lax.axis_index("col")
    swapped = (col_index != FIRST_COL) if by_col else False

    def dot(left, right):
        return jnp.dot(left, right, preferred_element_type=jnp.float32)

    def dot_t(left, right):
        return lax.dot_general(
            left, right, (((1,), (1,)), ((), ())), preferred_element_type=jnp.float32
        )

    def first_second(a_ref, b_ref, index):
        a_val, b_val = a_ref[index], b_ref[index]
        if not by_col:
            return a_val, b_val
        return jnp.where(swapped, b_val, a_val), jnp.where(swapped, a_val, b_val)

    upper = (
        lax.broadcasted_iota(jnp.int32, (PW, PW), 0) <= lax.broadcasted_iota(jnp.int32, (PW, PW), 1)
    )
    zero = jnp.zeros((PW, PW), jnp.bfloat16)
    upper_first = jnp.where(upper, inv_ref[0], zero)
    upper_second = jnp.where(upper, inv_ref[1], zero)

    slabs_first, slabs_second = first_second(
        pieces_a_ref, pieces_b_ref, (slice(None), slice(0, PW), slice(None))
    )
    flags_first, flags_second = first_second(
        pieces_a_ref, pieces_b_ref, (slice(None), slice(PW, PW + 1), slice(None))
    )
    diag_first = (
        dot(slabs_first.reshape(picks * PW, PW), upper_first).reshape(picks, PW, PW)
        * flags_first.astype(jnp.float32)
    ).astype(jnp.bfloat16)
    pivot = diag_first[col_panels]
    own_first = diag_first[:col_panels].reshape(col_panels * PW, PW)
    diag_update = (
        slabs_second[:col_panels].reshape(col_panels * PW, PW).astype(jnp.float32)
        - dot_t(own_first, pivot)
    ).astype(jnp.bfloat16)
    diag_second = (
        dot(diag_update, upper_second).reshape(col_panels, PW, PW)
        * flags_second[:col_panels].astype(jnp.float32)
    ).astype(jnp.bfloat16)

    cols_first, cols_second = first_second(cols_a_ref, cols_b_ref, slice(0, local_rows))
    rows_first, rows_second = first_second(
        cols_a_ref, cols_b_ref, slice(local_rows, local_rows + block_rows)
    )
    first_panel = (
        dot(cols_first, upper_first).reshape(block_rows, RB, PW)
        * rows_first.astype(jnp.float32)[:, None, :]
    ).astype(jnp.bfloat16).reshape(local_rows, PW)
    panel_update = (
        cols_second.astype(jnp.float32) - dot_t(first_panel, pivot)
    ).astype(jnp.bfloat16)
    second_panel = (
        dot(panel_update, upper_second).reshape(block_rows, RB, PW)
        * rows_second.astype(jnp.float32)[:, None, :]
    ).astype(jnp.bfloat16).reshape(local_rows, PW)
    both_panels = jnp.concatenate((first_panel, second_panel), axis=1)

    matrix_in.wait()
    panels_out = []
    for j in range(col_panels):
        cols = slice(j * PW, (j + 1) * PW)
        both_diag = jnp.concatenate((diag_first[j], diag_second[j]), axis=1)
        schur = matrix_ref[:, cols].astype(jnp.float32) - dot_t(both_panels, both_diag)
        for b in range(block_rows):
            rows = slice(b * RB, (b + 1) * RB)
            tile = (schur[rows] * mask_ref[b, j].astype(jnp.float32)).astype(jnp.bfloat16)
            if j == 0:
                tile = jnp.where(
                    col_index == FIRST_COL,
                    first_panel[rows],
                    jnp.where(col_index == SECOND_COL, second_panel[rows], tile),
                )
            out_ref[rows, cols] = tile
        copy = pltpu.make_async_copy(
            out_ref.at[:, pl.ds(j * PW, PW)], out_hbm.at[:, pl.ds(j * PW, PW)], sems.at[1 + j]
        )
        copy.start()
        panels_out.append(copy)
    for copy in panels_out:
        copy.wait()


def factor_call(matrix, cols_a, cols_b, pieces_a, pieces_b, inverses, fill_mask, by_col):
    local_rows, width = matrix.shape
    vmem = pl.BlockSpec(memory_space=pltpu.VMEM)
    smem = pl.BlockSpec(memory_space=pltpu.SMEM)
    flops = 2 * local_rows * width * 2 * PW + 6 * local_rows * PW * PW
    return pl.pallas_call(
        functools.partial(factor_kernel, by_col=by_col),
        out_shape=jax.ShapeDtypeStruct((local_rows, width), jnp.bfloat16),
        in_specs=[pl.BlockSpec(memory_space=pl.ANY)] + [vmem] * 5 + [smem],
        out_specs=pl.BlockSpec(memory_space=pl.ANY),
        scratch_shapes=[
            pltpu.VMEM((local_rows, width), jnp.bfloat16),
            pltpu.VMEM((local_rows, width), jnp.bfloat16),
            pltpu.SemaphoreType.DMA((1 + width // PW,)),
        ],
        cost_estimate=pl.CostEstimate(
            flops=flops, bytes_accessed=4 * local_rows * width, transcendentals=0
        ),
    )(matrix, cols_a, cols_b, pieces_a, pieces_b, inverses, fill_mask)


def solution(mesh):
    in_specs = (P("row", "col"), P("row", "col"), P(), P())
    out_specs = P("row", "col")
    return jax.shard_map(shards, mesh=mesh, in_specs=in_specs, out_specs=out_specs, check_vma=False)
```

```python
import functools

import jax
import jax.numpy as jnp
from jax import lax
from jax.experimental import pallas as pl
from jax.experimental.pallas import tpu as pltpu
from jax.sharding import PartitionSpec as P

RB = 256
PW = 128
FIRST_COL = 0
SECOND_COL = 1
MASK_ROWS = 16


def round_orders(bits):
    even = list(range(bits))[::-1]
    odd = list(even)
    for position in range(0, bits - 1, 2):
        odd[position], odd[position + 1] = odd[position + 1], odd[position]
    return even, odd


def gather_rows(piece, row_count, col_count):
    me = lax.axis_index("row")
    parity = lax.axis_index("col") % 2
    bits = row_count.bit_length() - 1
    even, odd = round_orders(bits)
    def exchange(value, masks):
        perm = []
        for r in range(row_count):
            for k in range(col_count):
                perm.append((r * col_count + k, (r ^ masks[k % 2]) * col_count + k))
        return lax.ppermute(value, ("row", "col"), perm)

    held = piece[None]
    for start in range(0, bits, 2):
        groups = ((start,), (start + 1,), (start, start + 1)) if start + 1 < bits else ((start,),)
        parts = [held]
        for chosen in groups:
            masks = [sum(1 << order[p] for p in chosen) for order in (even, odd)]
            parts.append(exchange(held, masks))
        held = jnp.concatenate(parts, axis=0)

    def slot_of(owner, order_parity):
        diff = jnp.bitwise_xor(owner, me)
        slot_even = jnp.zeros_like(diff)
        slot_odd = jnp.zeros_like(diff)
        for position in range(bits):
            slot_even = slot_even + ((diff >> even[position]) & 1) * (1 << position)
            slot_odd = slot_odd + ((diff >> odd[position]) & 1) * (1 << position)
        return jnp.where(order_parity == 0, slot_even, slot_odd)

    return held, slot_of, parity


def shards(matrix, fill_mask, col_rows, inverses):
    col_index = lax.axis_index("col")
    row_index = lax.axis_index("row")
    row_count = lax.axis_size("row")
    col_count = lax.axis_size("col")
    local_rows, width = matrix.shape
    col_panels = width // PW
    block_rows = local_rows // RB
    local_slabs = local_rows // PW

    owner_row = col_rows // local_slabs
    piece, payload = prep_call(matrix, col_rows, fill_mask)
    held, slot_of, parity = gather_rows(piece, row_count, col_count)

    def wanted_of(group):
        own = group * col_panels + jnp.arange(col_panels, dtype=jnp.int32)
        return jnp.concatenate((own, jnp.full((1,), SECOND_COL * col_panels, jnp.int32)))

    def pick(pieces, wanted, order_parity):
        slots = slot_of(owner_row[wanted], order_parity)
        return jnp.take(pieces, slots, axis=0)

    wanted = wanted_of(col_index)
    if col_count == 2:
        swap = [(0, 1), (1, 0)]
        cols_a = payload
        cols_b = lax.ppermute(payload, "col", swap)
        pieces_a = pick(held, wanted, parity)
        for_partner = pick(held, wanted_of(1 - col_index), parity)
        pieces_b = lax.ppermute(for_partner, "col", swap)
    else:
        lead = lax.all_gather(payload, "col", axis=0, tiled=False)
        cols_a, cols_b = lead[FIRST_COL], lead[SECOND_COL]
        everyone = lax.all_gather(held, "col", axis=0, tiled=False)
        pieces_a = pick(everyone[FIRST_COL], wanted, FIRST_COL % 2)
        pieces_b = pick(everyone[SECOND_COL], wanted, SECOND_COL % 2)

    return factor_call(
        matrix, cols_a, cols_b, pieces_a, pieces_b, inverses, fill_mask, col_count == 2
    )


def prep_kernel(lead_ref, col_rows_ref, mask_ref, piece_ref, payload_ref):
    local_rows = lead_ref.shape[0]
    local_slabs = local_rows // PW
    block_rows = local_rows // RB
    row_index = lax.axis_index("row")
    place = jnp.int32(0)
    for c in range(col_rows_ref.shape[0]):
        entry = col_rows_ref[c]
        place = place + jnp.where(entry // local_slabs == row_index, entry % local_slabs, 0)
    place = jnp.minimum(place, local_slabs - 1)
    start = pl.multiple_of(place * PW, PW)
    piece_ref[0:PW, :] = lead_ref[pl.ds(start, PW), :]
    flag = mask_ref[place // (RB // PW), 0].astype(jnp.float32)
    row_ids = lax.broadcasted_iota(jnp.int32, (MASK_ROWS, PW), 0)
    piece_ref[PW : PW + MASK_ROWS, :] = jnp.where(row_ids == 0, flag, 0.0).astype(jnp.bfloat16)
    payload_ref[0:local_rows, :] = lead_ref[...]
    mask_rows = jnp.zeros((MASK_ROWS, PW), jnp.float32)
    for b in range(block_rows):
        mask_rows = jnp.where(row_ids == b, mask_ref[b, 0].astype(jnp.float32), mask_rows)
    payload_ref[local_rows : local_rows + MASK_ROWS, :] = mask_rows.astype(jnp.bfloat16)


def prep_call(matrix, col_rows, fill_mask):
    local_rows = matrix.shape[0]
    smem = pl.BlockSpec(memory_space=pltpu.SMEM)
    return pl.pallas_call(
        prep_kernel,
        out_shape=(
            jax.ShapeDtypeStruct((PW + MASK_ROWS, PW), jnp.bfloat16),
            jax.ShapeDtypeStruct((local_rows + MASK_ROWS, PW), jnp.bfloat16),
        ),
        grid=(1,),
        in_specs=[pl.BlockSpec((local_rows, PW), lambda i: (0, 0)), smem, smem],
        out_specs=(
            pl.BlockSpec((PW + MASK_ROWS, PW), lambda i: (0, 0)),
            pl.BlockSpec((local_rows + MASK_ROWS, PW), lambda i: (0, 0)),
        ),
        cost_estimate=pl.CostEstimate(
            flops=0, bytes_accessed=4 * local_rows * PW, transcendentals=0
        ),
    )(matrix, col_rows, fill_mask)


def factor_kernel(
    matrix_ref, cols_a_ref, cols_b_ref, pieces_a_ref, pieces_b_ref, inv_ref, mask_ref, out_ref, *, by_col
):
    local_rows, width = matrix_ref.shape
    col_panels = width // PW
    block_rows = local_rows // RB
    picks = pieces_a_ref.shape[0]
    col_index = lax.axis_index("col")
    swapped = (col_index != FIRST_COL) if by_col else False

    def dot(left, right):
        return jnp.dot(left, right, preferred_element_type=jnp.float32)

    def dot_t(left, right):
        return lax.dot_general(
            left, right, (((1,), (1,)), ((), ())), preferred_element_type=jnp.float32
        )

    def first_second(a_ref, b_ref, index):
        a_val, b_val = a_ref[index], b_ref[index]
        if not by_col:
            return a_val, b_val
        return jnp.where(swapped, b_val, a_val), jnp.where(swapped, a_val, b_val)

    upper = (
        lax.broadcasted_iota(jnp.int32, (PW, PW), 0) <= lax.broadcasted_iota(jnp.int32, (PW, PW), 1)
    )
    zero = jnp.zeros((PW, PW), jnp.bfloat16)
    upper_first = jnp.where(upper, inv_ref[0], zero)
    upper_second = jnp.where(upper, inv_ref[1], zero)

    slabs_first, slabs_second = first_second(
        pieces_a_ref, pieces_b_ref, (slice(None), slice(0, PW), slice(None))
    )
    flags_first, flags_second = first_second(
        pieces_a_ref, pieces_b_ref, (slice(None), slice(PW, PW + 1), slice(None))
    )
    diag_first = (
        dot(slabs_first.reshape(picks * PW, PW), upper_first).reshape(picks, PW, PW)
        * flags_first.astype(jnp.float32)
    ).astype(jnp.bfloat16)
    pivot = diag_first[col_panels]
    own_first = diag_first[:col_panels].reshape(col_panels * PW, PW)
    diag_update = (
        slabs_second[:col_panels].reshape(col_panels * PW, PW).astype(jnp.float32)
        - dot_t(own_first, pivot)
    ).astype(jnp.bfloat16)
    diag_second = (
        dot(diag_update, upper_second).reshape(col_panels, PW, PW)
        * flags_second[:col_panels].astype(jnp.float32)
    ).astype(jnp.bfloat16)

    cols_first, cols_second = first_second(cols_a_ref, cols_b_ref, slice(0, local_rows))
    rows_first, rows_second = first_second(
        cols_a_ref, cols_b_ref, slice(local_rows, local_rows + block_rows)
    )
    first_panel = (
        dot(cols_first, upper_first).reshape(block_rows, RB, PW)
        * rows_first.astype(jnp.float32)[:, None, :]
    ).astype(jnp.bfloat16).reshape(local_rows, PW)
    panel_update = (
        cols_second.astype(jnp.float32) - dot_t(first_panel, pivot)
    ).astype(jnp.bfloat16)
    second_panel = (
        dot(panel_update, upper_second).reshape(block_rows, RB, PW)
        * rows_second.astype(jnp.float32)[:, None, :]
    ).astype(jnp.bfloat16).reshape(local_rows, PW)
    both_panels = jnp.concatenate((first_panel, second_panel), axis=1)

    leading = (col_index == FIRST_COL) | (col_index == SECOND_COL)
    for j in range(col_panels):
        cols = slice(j * PW, (j + 1) * PW)
        both_diag = jnp.concatenate((diag_first[j], diag_second[j]), axis=1)
        for b in range(block_rows):
            rows = slice(b * RB, (b + 1) * RB)
            scale = mask_ref[b, j]
            compute = scale != 0
            if j == 0:
                compute = compute & jnp.logical_not(leading)

                @pl.when(leading)
                def _(rows=rows, cols=cols):
                    out_ref[rows, cols] = jnp.where(
                        col_index == FIRST_COL, first_panel[rows], second_panel[rows]
                    )

            @pl.when(compute)
            def _(rows=rows, cols=cols, both_diag=both_diag, scale=scale):
                schur = matrix_ref[rows, cols].astype(jnp.float32) - dot_t(
                    both_panels[rows], both_diag
                )
                out_ref[rows, cols] = (schur * scale.astype(jnp.float32)).astype(jnp.bfloat16)

            skip = scale == 0
            if j == 0:
                skip = skip & jnp.logical_not(leading)

            @pl.when(skip)
            def _(rows=rows, cols=cols):
                out_ref[rows, cols] = jnp.zeros((RB, PW), jnp.bfloat16)


def factor_call(matrix, cols_a, cols_b, pieces_a, pieces_b, inverses, fill_mask, by_col):
    local_rows, width = matrix.shape
    vmem = pl.BlockSpec(memory_space=pltpu.VMEM)
    smem = pl.BlockSpec(memory_space=pltpu.SMEM)
    flops = 2 * local_rows * width * 2 * PW + 6 * local_rows * PW * PW
    return pl.pallas_call(
        functools.partial(factor_kernel, by_col=by_col),
        out_shape=jax.ShapeDtypeStruct((local_rows, width), jnp.bfloat16),
        in_specs=[vmem] * 6 + [smem],
        out_specs=vmem,
        cost_estimate=pl.CostEstimate(
            flops=flops, bytes_accessed=4 * local_rows * width, transcendentals=0
        ),
    )(matrix, cols_a, cols_b, pieces_a, pieces_b, inverses, fill_mask)


def solution(mesh):
    in_specs = (P("row", "col"), P("row", "col"), P(), P())
    out_specs = P("row", "col")
    return jax.shard_map(shards, mesh=mesh, in_specs=in_specs, out_specs=out_specs, check_vma=False)
```

```python
import functools

import jax
import jax.numpy as jnp
from jax import lax
from jax.experimental import pallas as pl
from jax.experimental.pallas import tpu as pltpu
from jax.sharding import PartitionSpec as P

RB = 256
PW = 128
FIRST_COL = 0
SECOND_COL = 1
MASK_ROWS = 16


def round_orders(bits):
    even = list(range(bits))[::-1]
    odd = list(even)
    for position in range(0, bits - 1, 2):
        odd[position], odd[position + 1] = odd[position + 1], odd[position]
    return even, odd


def gather_rows(piece, row_count, col_count):
    me = lax.axis_index("row")
    parity = lax.axis_index("col") % 2
    bits = row_count.bit_length() - 1
    even, odd = round_orders(bits)
    def exchange(value, masks):
        perm = []
        for r in range(row_count):
            for k in range(col_count):
                perm.append((r * col_count + k, (r ^ masks[k % 2]) * col_count + k))
        return lax.ppermute(value, ("row", "col"), perm)

    held = piece[None]
    for start in range(0, bits, 2):
        groups = ((start,), (start + 1,), (start, start + 1)) if start + 1 < bits else ((start,),)
        parts = [held]
        for chosen in groups:
            masks = [sum(1 << order[p] for p in chosen) for order in (even, odd)]
            parts.append(exchange(held, masks))
        held = jnp.concatenate(parts, axis=0)

    def slot_of(owner, order_parity):
        diff = jnp.bitwise_xor(owner, me)
        slot_even = jnp.zeros_like(diff)
        slot_odd = jnp.zeros_like(diff)
        for position in range(bits):
            slot_even = slot_even + ((diff >> even[position]) & 1) * (1 << position)
            slot_odd = slot_odd + ((diff >> odd[position]) & 1) * (1 << position)
        return jnp.where(order_parity == 0, slot_even, slot_odd)

    return held, slot_of, parity


def shards(matrix, fill_mask, col_rows, inverses):
    col_index = lax.axis_index("col")
    row_index = lax.axis_index("row")
    row_count = lax.axis_size("row")
    col_count = lax.axis_size("col")
    local_rows, width = matrix.shape
    col_panels = width // PW
    block_rows = local_rows // RB
    local_slabs = local_rows // PW

    owner_row = col_rows // local_slabs
    piece, payload = prep_call(matrix, col_rows, fill_mask)
    held, slot_of, parity = gather_rows(piece, row_count, col_count)

    def wanted_of(group):
        own = group * col_panels + jnp.arange(col_panels, dtype=jnp.int32)
        return jnp.concatenate((own, jnp.full((1,), SECOND_COL * col_panels, jnp.int32)))

    def pick(pieces, wanted, order_parity):
        slots = slot_of(owner_row[wanted], order_parity)
        return jnp.take(pieces, slots, axis=0)

    wanted = wanted_of(col_index)
    if col_count == 2:
        swap = [(0, 1), (1, 0)]
        cols_a = payload
        cols_b = lax.ppermute(payload, "col", swap)
        pieces_a = pick(held, wanted, parity)
        for_partner = pick(held, wanted_of(1 - col_index), parity)
        pieces_b = lax.ppermute(for_partner, "col", swap)
    else:
        lead = lax.all_gather(payload, "col", axis=0, tiled=False)
        cols_a, cols_b = lead[FIRST_COL], lead[SECOND_COL]
        everyone = lax.all_gather(held, "col", axis=0, tiled=False)
        pieces_a = pick(everyone[FIRST_COL], wanted, FIRST_COL % 2)
        pieces_b = pick(everyone[SECOND_COL], wanted, SECOND_COL % 2)

    return factor_call(
        matrix, cols_a, cols_b, pieces_a, pieces_b, inverses, fill_mask, col_count == 2
    )


def prep_kernel(lead_ref, col_rows_ref, mask_ref, piece_ref, payload_ref):
    local_rows = lead_ref.shape[0]
    local_slabs = local_rows // PW
    block_rows = local_rows // RB
    row_index = lax.axis_index("row")
    place = jnp.int32(0)
    for c in range(col_rows_ref.shape[0]):
        entry = col_rows_ref[c]
        place = place + jnp.where(entry // local_slabs == row_index, entry % local_slabs, 0)
    place = jnp.minimum(place, local_slabs - 1)
    start = pl.multiple_of(place * PW, PW)
    piece_ref[0:PW, :] = lead_ref[pl.ds(start, PW), :]
    flag = mask_ref[place // (RB // PW), 0].astype(jnp.float32)
    row_ids = lax.broadcasted_iota(jnp.int32, (MASK_ROWS, PW), 0)
    piece_ref[PW : PW + MASK_ROWS, :] = jnp.where(row_ids == 0, flag, 0.0).astype(jnp.bfloat16)
    payload_ref[0:local_rows, :] = lead_ref[...]
    mask_rows = jnp.zeros((MASK_ROWS, PW), jnp.float32)
    for b in range(block_rows):
        mask_rows = jnp.where(row_ids == b, mask_ref[b, 0].astype(jnp.float32), mask_rows)
    payload_ref[local_rows : local_rows + MASK_ROWS, :] = mask_rows.astype(jnp.bfloat16)


def prep_call(matrix, col_rows, fill_mask):
    local_rows = matrix.shape[0]
    smem = pl.BlockSpec(memory_space=pltpu.SMEM)
    return pl.pallas_call(
        prep_kernel,
        out_shape=(
            jax.ShapeDtypeStruct((PW + MASK_ROWS, PW), jnp.bfloat16),
            jax.ShapeDtypeStruct((local_rows + MASK_ROWS, PW), jnp.bfloat16),
        ),
        grid=(1,),
        in_specs=[pl.BlockSpec((local_rows, PW), lambda i: (0, 0)), smem, smem],
        out_specs=(
            pl.BlockSpec((PW + MASK_ROWS, PW), lambda i: (0, 0)),
            pl.BlockSpec((local_rows + MASK_ROWS, PW), lambda i: (0, 0)),
        ),
        cost_estimate=pl.CostEstimate(
            flops=0, bytes_accessed=4 * local_rows * PW, transcendentals=0
        ),
    )(matrix, col_rows, fill_mask)


def factor_kernel(
    matrix_ref, cols_a_ref, cols_b_ref, pieces_a_ref, pieces_b_ref, inv_ref, mask_ref, out_ref, *, by_col
):
    local_rows, width = matrix_ref.shape
    col_panels = width // PW
    block_rows = local_rows // RB
    picks = pieces_a_ref.shape[0]
    col_index = lax.axis_index("col")
    swapped = (col_index != FIRST_COL) if by_col else False

    def dot(left, right):
        return jnp.dot(left, right, preferred_element_type=jnp.float32)

    def dot_t(left, right):
        return lax.dot_general(
            left, right, (((1,), (1,)), ((), ())), preferred_element_type=jnp.float32
        )

    def first_second(a_ref, b_ref, index):
        a_val, b_val = a_ref[index], b_ref[index]
        if not by_col:
            return a_val, b_val
        return jnp.where(swapped, b_val, a_val), jnp.where(swapped, a_val, b_val)

    upper = (
        lax.broadcasted_iota(jnp.int32, (PW, PW), 0) <= lax.broadcasted_iota(jnp.int32, (PW, PW), 1)
    )
    zero = jnp.zeros((PW, PW), jnp.bfloat16)
    upper_first = jnp.where(upper, inv_ref[0], zero)
    upper_second = jnp.where(upper, inv_ref[1], zero)

    slabs_first, slabs_second = first_second(
        pieces_a_ref, pieces_b_ref, (slice(None), slice(0, PW), slice(None))
    )
    flags_first, flags_second = first_second(
        pieces_a_ref, pieces_b_ref, (slice(None), slice(PW, PW + 1), slice(None))
    )
    diag_first = (
        dot(slabs_first.reshape(picks * PW, PW), upper_first).reshape(picks, PW, PW)
        * flags_first.astype(jnp.float32)
    ).astype(jnp.bfloat16)
    pivot = diag_first[col_panels]
    own_first = diag_first[:col_panels].reshape(col_panels * PW, PW)
    diag_update = (
        slabs_second[:col_panels].reshape(col_panels * PW, PW).astype(jnp.float32)
        - dot_t(own_first, pivot)
    ).astype(jnp.bfloat16)
    diag_second = (
        dot(diag_update, upper_second).reshape(col_panels, PW, PW)
        * flags_second[:col_panels].astype(jnp.float32)
    ).astype(jnp.bfloat16)

    cols_first, cols_second = first_second(cols_a_ref, cols_b_ref, slice(0, local_rows))
    rows_first, rows_second = first_second(
        cols_a_ref, cols_b_ref, slice(local_rows, local_rows + block_rows)
    )
    first_panel = (
        dot(cols_first, upper_first).reshape(block_rows, RB, PW)
        * rows_first.astype(jnp.float32)[:, None, :]
    ).astype(jnp.bfloat16).reshape(local_rows, PW)
    panel_update = (
        cols_second.astype(jnp.float32) - dot_t(first_panel, pivot)
    ).astype(jnp.bfloat16)
    second_panel = (
        dot(panel_update, upper_second).reshape(block_rows, RB, PW)
        * rows_second.astype(jnp.float32)[:, None, :]
    ).astype(jnp.bfloat16).reshape(local_rows, PW)
    both_panels = jnp.concatenate((first_panel, second_panel), axis=1)

    all_diag = jnp.concatenate(
        (diag_first[:col_panels].reshape(width, PW), diag_second.reshape(width, PW)), axis=1
    )
    product = dot_t(both_panels, all_diag)
    lane_panel = lax.broadcasted_iota(jnp.int32, (1, width), 1) // PW
    for b in range(block_rows):
        rows = slice(b * RB, (b + 1) * RB)
        scale = jnp.zeros((1, width), jnp.float32)
        for j in range(col_panels):
            scale = jnp.where(lane_panel == j, mask_ref[b, j].astype(jnp.float32), scale)
        schur = matrix_ref[rows, :].astype(jnp.float32) - product[rows]
        out_ref[rows, :] = (schur * scale).astype(jnp.bfloat16)
        lead = out_ref[rows, 0:PW]
        out_ref[rows, 0:PW] = jnp.where(
            col_index == FIRST_COL,
            first_panel[rows],
            jnp.where(col_index == SECOND_COL, second_panel[rows], lead),
        )


def factor_call(matrix, cols_a, cols_b, pieces_a, pieces_b, inverses, fill_mask, by_col):
    local_rows, width = matrix.shape
    vmem = pl.BlockSpec(memory_space=pltpu.VMEM)
    smem = pl.BlockSpec(memory_space=pltpu.SMEM)
    flops = 2 * local_rows * width * 2 * PW + 6 * local_rows * PW * PW
    return pl.pallas_call(
        functools.partial(factor_kernel, by_col=by_col),
        out_shape=jax.ShapeDtypeStruct((local_rows, width), jnp.bfloat16),
        in_specs=[vmem] * 6 + [smem],
        out_specs=vmem,
        cost_estimate=pl.CostEstimate(
            flops=flops, bytes_accessed=4 * local_rows * width, transcendentals=0
        ),
    )(matrix, cols_a, cols_b, pieces_a, pieces_b, inverses, fill_mask)


def solution(mesh):
    in_specs = (P("row", "col"), P("row", "col"), P(), P())
    out_specs = P("row", "col")
    return jax.shard_map(shards, mesh=mesh, in_specs=in_specs, out_specs=out_specs, check_vma=False)
```

```python
import functools

import jax
import jax.numpy as jnp
from jax import lax
from jax.experimental import pallas as pl
from jax.experimental.pallas import tpu as pltpu
from jax.sharding import PartitionSpec as P

RB = 256
PW = 128
FIRST_COL = 0
SECOND_COL = 1
MASK_ROWS = 16


def round_orders(bits):
    even = list(range(bits))[::-1]
    odd = list(even)
    for position in range(0, bits - 1, 2):
        odd[position], odd[position + 1] = odd[position + 1], odd[position]
    return even, odd


def gather_rows(piece, row_count, col_count):
    me = lax.axis_index("row")
    parity = lax.axis_index("col") % 2
    bits = row_count.bit_length() - 1
    even, odd = round_orders(bits)
    def exchange(value, masks):
        perm = []
        for r in range(row_count):
            for k in range(col_count):
                perm.append((r * col_count + k, (r ^ masks[k % 2]) * col_count + k))
        return lax.ppermute(value, ("row", "col"), perm)

    held = piece[None]
    for start in range(0, bits, 2):
        groups = ((start,), (start + 1,), (start, start + 1)) if start + 1 < bits else ((start,),)
        parts = [held]
        for chosen in groups:
            masks = [sum(1 << order[p] for p in chosen) for order in (even, odd)]
            parts.append(exchange(held, masks))
        held = jnp.concatenate(parts, axis=0)

    def slot_of(owner, order_parity):
        diff = jnp.bitwise_xor(owner, me)
        slot_even = jnp.zeros_like(diff)
        slot_odd = jnp.zeros_like(diff)
        for position in range(bits):
            slot_even = slot_even + ((diff >> even[position]) & 1) * (1 << position)
            slot_odd = slot_odd + ((diff >> odd[position]) & 1) * (1 << position)
        return jnp.where(order_parity == 0, slot_even, slot_odd)

    return held, slot_of, parity


def shards(matrix, fill_mask, col_rows, inverses):
    col_index = lax.axis_index("col")
    row_index = lax.axis_index("row")
    row_count = lax.axis_size("row")
    col_count = lax.axis_size("col")
    local_rows, width = matrix.shape
    col_panels = width // PW
    block_rows = local_rows // RB
    local_slabs = local_rows // PW

    owner_row = col_rows // local_slabs
    piece, payload = prep_call(matrix, col_rows, fill_mask)
    held, slot_of, parity = gather_rows(piece, row_count, col_count)

    def wanted_of(group):
        own = group * col_panels + jnp.arange(col_panels, dtype=jnp.int32)
        return jnp.concatenate((own, jnp.full((1,), SECOND_COL * col_panels, jnp.int32)))

    def pick(pieces, wanted, order_parity):
        slots = slot_of(owner_row[wanted], order_parity)
        return jnp.take(pieces, slots, axis=0)

    wanted = wanted_of(col_index)
    if col_count == 2:
        swap = [(0, 1), (1, 0)]
        cols_a = payload
        cols_b = lax.ppermute(payload, "col", swap)
        pieces_a = pick(held, wanted, parity)
        for_partner = pick(held, wanted_of(1 - col_index), parity)
        pieces_b = lax.ppermute(for_partner, "col", swap)
    else:
        lead = lax.all_gather(payload, "col", axis=0, tiled=False)
        cols_a, cols_b = lead[FIRST_COL], lead[SECOND_COL]
        everyone = lax.all_gather(held, "col", axis=0, tiled=False)
        pieces_a = pick(everyone[FIRST_COL], wanted, FIRST_COL % 2)
        pieces_b = pick(everyone[SECOND_COL], wanted, SECOND_COL % 2)

    return factor_call(
        matrix, cols_a, cols_b, pieces_a, pieces_b, inverses, fill_mask, col_count == 2
    )


def prep_kernel(lead_ref, col_rows_ref, mask_ref, piece_ref, payload_ref):
    local_rows = lead_ref.shape[0]
    local_slabs = local_rows // PW
    block_rows = local_rows // RB
    row_index = lax.axis_index("row")
    place = jnp.int32(0)
    for c in range(col_rows_ref.shape[0]):
        entry = col_rows_ref[c]
        place = place + jnp.where(entry // local_slabs == row_index, entry % local_slabs, 0)
    place = jnp.minimum(place, local_slabs - 1)
    start = pl.multiple_of(place * PW, PW)
    piece_ref[0:PW, :] = lead_ref[pl.ds(start, PW), :]
    flag = mask_ref[place // (RB // PW), 0].astype(jnp.float32)
    row_ids = lax.broadcasted_iota(jnp.int32, (MASK_ROWS, PW), 0)
    piece_ref[PW : PW + MASK_ROWS, :] = jnp.where(row_ids == 0, flag, 0.0).astype(jnp.bfloat16)
    payload_ref[0:local_rows, :] = lead_ref[...]
    mask_rows = jnp.zeros((MASK_ROWS, PW), jnp.float32)
    for b in range(block_rows):
        mask_rows = jnp.where(row_ids == b, mask_ref[b, 0].astype(jnp.float32), mask_rows)
    payload_ref[local_rows : local_rows + MASK_ROWS, :] = mask_rows.astype(jnp.bfloat16)


def prep_call(matrix, col_rows, fill_mask):
    local_rows = matrix.shape[0]
    smem = pl.BlockSpec(memory_space=pltpu.SMEM)
    return pl.pallas_call(
        prep_kernel,
        out_shape=(
            jax.ShapeDtypeStruct((PW + MASK_ROWS, PW), jnp.bfloat16),
            jax.ShapeDtypeStruct((local_rows + MASK_ROWS, PW), jnp.bfloat16),
        ),
        grid=(1,),
        in_specs=[pl.BlockSpec((local_rows, PW), lambda i: (0, 0)), smem, smem],
        out_specs=(
            pl.BlockSpec((PW + MASK_ROWS, PW), lambda i: (0, 0)),
            pl.BlockSpec((local_rows + MASK_ROWS, PW), lambda i: (0, 0)),
        ),
        cost_estimate=pl.CostEstimate(
            flops=0, bytes_accessed=4 * local_rows * PW, transcendentals=0
        ),
    )(matrix, col_rows, fill_mask)


def factor_kernel(
    matrix_ref, cols_a_ref, cols_b_ref, pieces_a_ref, pieces_b_ref, inv_ref, mask_ref, out_ref, *, by_col
):
    local_rows, width = matrix_ref.shape
    col_panels = width // PW
    block_rows = local_rows // RB
    picks = pieces_a_ref.shape[0]
    col_index = lax.axis_index("col")
    swapped = (col_index != FIRST_COL) if by_col else False

    def dot(left, right):
        return jnp.dot(left, right, preferred_element_type=jnp.float32)

    def dot_t(left, right):
        return lax.dot_general(
            left, right, (((1,), (1,)), ((), ())), preferred_element_type=jnp.float32
        )

    def first_second(a_ref, b_ref, index):
        a_val, b_val = a_ref[index], b_ref[index]
        if not by_col:
            return a_val, b_val
        return jnp.where(swapped, b_val, a_val), jnp.where(swapped, a_val, b_val)

    upper = (
        lax.broadcasted_iota(jnp.int32, (PW, PW), 0) <= lax.broadcasted_iota(jnp.int32, (PW, PW), 1)
    )
    zero = jnp.zeros((PW, PW), jnp.bfloat16)
    upper_first = jnp.where(upper, inv_ref[0], zero)
    upper_second = jnp.where(upper, inv_ref[1], zero)

    slabs_first, slabs_second = first_second(
        pieces_a_ref, pieces_b_ref, (slice(None), slice(0, PW), slice(None))
    )
    flags_first, flags_second = first_second(
        pieces_a_ref, pieces_b_ref, (slice(None), slice(PW, PW + 1), slice(None))
    )
    cols_first, cols_second = first_second(cols_a_ref, cols_b_ref, slice(0, local_rows))
    rows_first, rows_second = first_second(
        cols_a_ref, cols_b_ref, slice(local_rows, local_rows + block_rows)
    )
    diag_rows = picks * PW
    own_rows = col_panels * PW
    scale_first = jnp.concatenate(
        (
            jnp.broadcast_to(flags_first.astype(jnp.float32), (picks, PW, PW)).reshape(diag_rows, PW),
            jnp.broadcast_to(rows_first.astype(jnp.float32)[:, None, :], (block_rows, RB, PW)).reshape(
                local_rows, PW
            ),
        ),
        axis=0,
    )
    stacked_first = (
        dot(jnp.concatenate((slabs_first.reshape(diag_rows, PW), cols_first), axis=0), upper_first)
        * scale_first
    ).astype(jnp.bfloat16)
    diag_first = stacked_first[:diag_rows].reshape(picks, PW, PW)
    first_panel = stacked_first[diag_rows:]
    pivot = diag_first[col_panels]
    stacked_left = jnp.concatenate((stacked_first[:own_rows], first_panel), axis=0)
    stacked_raw = jnp.concatenate(
        (slabs_second[:col_panels].reshape(own_rows, PW), cols_second), axis=0
    )
    stacked_update = (
        stacked_raw.astype(jnp.float32) - dot_t(stacked_left, pivot)
    ).astype(jnp.bfloat16)
    scale_second = jnp.concatenate(
        (
            jnp.broadcast_to(
                flags_second[:col_panels].astype(jnp.float32), (col_panels, PW, PW)
            ).reshape(own_rows, PW),
            jnp.broadcast_to(rows_second.astype(jnp.float32)[:, None, :], (block_rows, RB, PW)).reshape(
                local_rows, PW
            ),
        ),
        axis=0,
    )
    stacked_second = (dot(stacked_update, upper_second) * scale_second).astype(jnp.bfloat16)
    diag_second = stacked_second[:own_rows].reshape(col_panels, PW, PW)
    second_panel = stacked_second[own_rows:]
    both_panels = jnp.concatenate((first_panel, second_panel), axis=1)

    all_diag = jnp.concatenate(
        (diag_first[:col_panels].reshape(width, PW), diag_second.reshape(width, PW)), axis=1
    )
    product = dot_t(both_panels, all_diag)
    lane_panel = lax.broadcasted_iota(jnp.int32, (1, width), 1) // PW
    for b in range(block_rows):
        rows = slice(b * RB, (b + 1) * RB)
        scale = jnp.zeros((1, width), jnp.float32)
        for j in range(col_panels):
            scale = jnp.where(lane_panel == j, mask_ref[b, j].astype(jnp.float32), scale)
        schur = matrix_ref[rows, :].astype(jnp.float32) - product[rows]
        out_ref[rows, :] = (schur * scale).astype(jnp.bfloat16)
        lead = out_ref[rows, 0:PW]
        out_ref[rows, 0:PW] = jnp.where(
            col_index == FIRST_COL,
            first_panel[rows],
            jnp.where(col_index == SECOND_COL, second_panel[rows], lead),
        )


def factor_call(matrix, cols_a, cols_b, pieces_a, pieces_b, inverses, fill_mask, by_col):
    local_rows, width = matrix.shape
    vmem = pl.BlockSpec(memory_space=pltpu.VMEM)
    smem = pl.BlockSpec(memory_space=pltpu.SMEM)
    flops = 2 * local_rows * width * 2 * PW + 6 * local_rows * PW * PW
    return pl.pallas_call(
        functools.partial(factor_kernel, by_col=by_col),
        out_shape=jax.ShapeDtypeStruct((local_rows, width), jnp.bfloat16),
        in_specs=[vmem] * 6 + [smem],
        out_specs=vmem,
        cost_estimate=pl.CostEstimate(
            flops=flops, bytes_accessed=4 * local_rows * width, transcendentals=0
        ),
    )(matrix, cols_a, cols_b, pieces_a, pieces_b, inverses, fill_mask)


def solution(mesh):
    in_specs = (P("row", "col"), P("row", "col"), P(), P())
    out_specs = P("row", "col")
    return jax.shard_map(shards, mesh=mesh, in_specs=in_specs, out_specs=out_specs, check_vma=False)
```

```python
import functools

import jax
import jax.numpy as jnp
from jax import lax
from jax.experimental import pallas as pl
from jax.experimental.pallas import tpu as pltpu
from jax.sharding import PartitionSpec as P

RB = 256
PW = 128
FIRST_COL = 0
SECOND_COL = 1
MASK_ROWS = 16


def round_orders(bits):
    even = list(range(bits))[::-1]
    odd = list(even)
    for position in range(0, bits - 1, 2):
        odd[position], odd[position + 1] = odd[position + 1], odd[position]
    return even, odd


def gather_rows(piece, row_count, col_count, companion):
    me = lax.axis_index("row")
    parity = lax.axis_index("col") % 2
    bits = row_count.bit_length() - 1
    even, odd = round_orders(bits)
    def exchange(value, masks):
        perm = []
        for r in range(row_count):
            for k in range(col_count):
                perm.append((r * col_count + k, (r ^ masks[k % 2]) * col_count + k))
        return lax.ppermute(value, ("row", "col"), perm)

    held = piece[None]
    for start in range(0, bits, 2):
        groups = ((start,), (start + 1,), (start, start + 1)) if start + 1 < bits else ((start,),)
        parts = [held]
        for chosen in groups:
            masks = [sum(1 << order[p] for p in chosen) for order in (even, odd)]
            parts.append(exchange(held, masks))
        held = jnp.concatenate(parts, axis=0)
        if start == 0:
            held, companion = lax.optimization_barrier((held, companion))

    def slot_of(owner, order_parity):
        diff = jnp.bitwise_xor(owner, me)
        slot_even = jnp.zeros_like(diff)
        slot_odd = jnp.zeros_like(diff)
        for position in range(bits):
            slot_even = slot_even + ((diff >> even[position]) & 1) * (1 << position)
            slot_odd = slot_odd + ((diff >> odd[position]) & 1) * (1 << position)
        return jnp.where(order_parity == 0, slot_even, slot_odd)

    return held, slot_of, parity, companion


def shards(matrix, fill_mask, col_rows, inverses):
    col_index = lax.axis_index("col")
    row_index = lax.axis_index("row")
    row_count = lax.axis_size("row")
    col_count = lax.axis_size("col")
    local_rows, width = matrix.shape
    col_panels = width // PW
    block_rows = local_rows // RB
    local_slabs = local_rows // PW

    owner_row = col_rows // local_slabs
    piece, payload = prep_call(matrix, col_rows, fill_mask)
    if col_count == 2:
        swap = [(0, 1), (1, 0)]
        swapped_cols = lax.ppermute(payload, "col", swap)
    else:
        swapped_cols = payload
    held, slot_of, parity, swapped_cols = gather_rows(piece, row_count, col_count, swapped_cols)

    def wanted_of(group):
        own = group * col_panels + jnp.arange(col_panels, dtype=jnp.int32)
        return jnp.concatenate((own, jnp.full((1,), SECOND_COL * col_panels, jnp.int32)))

    def pick(pieces, wanted, order_parity):
        slots = slot_of(owner_row[wanted], order_parity)
        return jnp.take(pieces, slots, axis=0)

    wanted = wanted_of(col_index)
    if col_count == 2:
        cols_a = payload
        cols_b = swapped_cols
        pieces_a = pick(held, wanted, parity)
        for_partner = pick(held, wanted_of(1 - col_index), parity)
        pieces_b = lax.ppermute(for_partner, "col", swap)
    else:
        lead = lax.all_gather(payload, "col", axis=0, tiled=False)
        cols_a, cols_b = lead[FIRST_COL], lead[SECOND_COL]
        everyone = lax.all_gather(held, "col", axis=0, tiled=False)
        pieces_a = pick(everyone[FIRST_COL], wanted, FIRST_COL % 2)
        pieces_b = pick(everyone[SECOND_COL], wanted, SECOND_COL % 2)

    return factor_call(
        matrix, cols_a, cols_b, pieces_a, pieces_b, inverses, fill_mask, col_count == 2
    )


def prep_kernel(lead_ref, col_rows_ref, mask_ref, piece_ref, payload_ref):
    local_rows = lead_ref.shape[0]
    local_slabs = local_rows // PW
    block_rows = local_rows // RB
    row_index = lax.axis_index("row")
    place = jnp.int32(0)
    for c in range(col_rows_ref.shape[0]):
        entry = col_rows_ref[c]
        place = place + jnp.where(entry // local_slabs == row_index, entry % local_slabs, 0)
    place = jnp.minimum(place, local_slabs - 1)
    start = pl.multiple_of(place * PW, PW)
    piece_ref[0:PW, :] = lead_ref[pl.ds(start, PW), :]
    flag = mask_ref[place // (RB // PW), 0].astype(jnp.float32)
    row_ids = lax.broadcasted_iota(jnp.int32, (MASK_ROWS, PW), 0)
    piece_ref[PW : PW + MASK_ROWS, :] = jnp.where(row_ids == 0, flag, 0.0).astype(jnp.bfloat16)
    payload_ref[0:local_rows, :] = lead_ref[...]
    mask_rows = jnp.zeros((MASK_ROWS, PW), jnp.float32)
    for b in range(block_rows):
        mask_rows = jnp.where(row_ids == b, mask_ref[b, 0].astype(jnp.float32), mask_rows)
    payload_ref[local_rows : local_rows + MASK_ROWS, :] = mask_rows.astype(jnp.bfloat16)


def prep_call(matrix, col_rows, fill_mask):
    local_rows = matrix.shape[0]
    smem = pl.BlockSpec(memory_space=pltpu.SMEM)
    return pl.pallas_call(
        prep_kernel,
        out_shape=(
            jax.ShapeDtypeStruct((PW + MASK_ROWS, PW), jnp.bfloat16),
            jax.ShapeDtypeStruct((local_rows + MASK_ROWS, PW), jnp.bfloat16),
        ),
        grid=(1,),
        in_specs=[pl.BlockSpec((local_rows, PW), lambda i: (0, 0)), smem, smem],
        out_specs=(
            pl.BlockSpec((PW + MASK_ROWS, PW), lambda i: (0, 0)),
            pl.BlockSpec((local_rows + MASK_ROWS, PW), lambda i: (0, 0)),
        ),
        cost_estimate=pl.CostEstimate(
            flops=0, bytes_accessed=4 * local_rows * PW, transcendentals=0
        ),
    )(matrix, col_rows, fill_mask)


def factor_kernel(
    matrix_ref, cols_a_ref, cols_b_ref, pieces_a_ref, pieces_b_ref, inv_ref, mask_ref, out_ref, *, by_col
):
    local_rows, width = matrix_ref.shape
    col_panels = width // PW
    block_rows = local_rows // RB
    picks = pieces_a_ref.shape[0]
    col_index = lax.axis_index("col")
    swapped = (col_index != FIRST_COL) if by_col else False

    def dot(left, right):
        return jnp.dot(left, right, preferred_element_type=jnp.float32)

    def dot_t(left, right):
        return lax.dot_general(
            left, right, (((1,), (1,)), ((), ())), preferred_element_type=jnp.float32
        )

    def first_second(a_ref, b_ref, index):
        a_val, b_val = a_ref[index], b_ref[index]
        if not by_col:
            return a_val, b_val
        return jnp.where(swapped, b_val, a_val), jnp.where(swapped, a_val, b_val)

    upper = (
        lax.broadcasted_iota(jnp.int32, (PW, PW), 0) <= lax.broadcasted_iota(jnp.int32, (PW, PW), 1)
    )
    zero = jnp.zeros((PW, PW), jnp.bfloat16)
    upper_first = jnp.where(upper, inv_ref[0], zero)
    upper_second = jnp.where(upper, inv_ref[1], zero)

    slabs_first, slabs_second = first_second(
        pieces_a_ref, pieces_b_ref, (slice(None), slice(0, PW), slice(None))
    )
    flags_first, flags_second = first_second(
        pieces_a_ref, pieces_b_ref, (slice(None), slice(PW, PW + 1), slice(None))
    )
    diag_first = (
        dot(slabs_first.reshape(picks * PW, PW), upper_first).reshape(picks, PW, PW)
        * flags_first.astype(jnp.float32)
    ).astype(jnp.bfloat16)
    pivot = diag_first[col_panels]
    own_first = diag_first[:col_panels].reshape(col_panels * PW, PW)
    diag_update = (
        slabs_second[:col_panels].reshape(col_panels * PW, PW).astype(jnp.float32)
        - dot_t(own_first, pivot)
    ).astype(jnp.bfloat16)
    diag_second = (
        dot(diag_update, upper_second).reshape(col_panels, PW, PW)
        * flags_second[:col_panels].astype(jnp.float32)
    ).astype(jnp.bfloat16)

    cols_first, cols_second = first_second(cols_a_ref, cols_b_ref, slice(0, local_rows))
    rows_first, rows_second = first_second(
        cols_a_ref, cols_b_ref, slice(local_rows, local_rows + block_rows)
    )
    first_panel = (
        dot(cols_first, upper_first).reshape(block_rows, RB, PW)
        * rows_first.astype(jnp.float32)[:, None, :]
    ).astype(jnp.bfloat16).reshape(local_rows, PW)
    panel_update = (
        cols_second.astype(jnp.float32) - dot_t(first_panel, pivot)
    ).astype(jnp.bfloat16)
    second_panel = (
        dot(panel_update, upper_second).reshape(block_rows, RB, PW)
        * rows_second.astype(jnp.float32)[:, None, :]
    ).astype(jnp.bfloat16).reshape(local_rows, PW)
    both_panels = jnp.concatenate((first_panel, second_panel), axis=1)

    all_diag = jnp.concatenate(
        (diag_first[:col_panels].reshape(width, PW), diag_second.reshape(width, PW)), axis=1
    )
    product = dot_t(both_panels, all_diag)
    lane_panel = lax.broadcasted_iota(jnp.int32, (1, width), 1) // PW
    for b in range(block_rows):
        rows = slice(b * RB, (b + 1) * RB)
        scale = jnp.zeros((1, width), jnp.float32)
        for j in range(col_panels):
            scale = jnp.where(lane_panel == j, mask_ref[b, j].astype(jnp.float32), scale)
        schur = matrix_ref[rows, :].astype(jnp.float32) - product[rows]
        out_ref[rows, :] = (schur * scale).astype(jnp.bfloat16)
        lead = out_ref[rows, 0:PW]
        out_ref[rows, 0:PW] = jnp.where(
            col_index == FIRST_COL,
            first_panel[rows],
            jnp.where(col_index == SECOND_COL, second_panel[rows], lead),
        )


def factor_call(matrix, cols_a, cols_b, pieces_a, pieces_b, inverses, fill_mask, by_col):
    local_rows, width = matrix.shape
    vmem = pl.BlockSpec(memory_space=pltpu.VMEM)
    smem = pl.BlockSpec(memory_space=pltpu.SMEM)
    flops = 2 * local_rows * width * 2 * PW + 6 * local_rows * PW * PW
    return pl.pallas_call(
        functools.partial(factor_kernel, by_col=by_col),
        out_shape=jax.ShapeDtypeStruct((local_rows, width), jnp.bfloat16),
        in_specs=[vmem] * 6 + [smem],
        out_specs=vmem,
        cost_estimate=pl.CostEstimate(
            flops=flops, bytes_accessed=4 * local_rows * width, transcendentals=0
        ),
    )(matrix, cols_a, cols_b, pieces_a, pieces_b, inverses, fill_mask)


def solution(mesh):
    in_specs = (P("row", "col"), P("row", "col"), P(), P())
    out_specs = P("row", "col")
    return jax.shard_map(shards, mesh=mesh, in_specs=in_specs, out_specs=out_specs, check_vma=False)
```

```python
import functools

import jax
import jax.numpy as jnp
from jax import lax
from jax.experimental import pallas as pl
from jax.experimental.pallas import tpu as pltpu
from jax.sharding import PartitionSpec as P

RB = 256
PW = 128
FIRST_COL = 0
SECOND_COL = 1
MASK_ROWS = 16


def round_orders(bits):
    even = list(range(bits))[::-1]
    odd = list(even)
    for position in range(0, bits - 1, 2):
        odd[position], odd[position + 1] = odd[position + 1], odd[position]
    return even, odd


def gather_rows(piece, row_count, col_count):
    me = lax.axis_index("row")
    parity = lax.axis_index("col") % 2
    bits = row_count.bit_length() - 1
    even, odd = round_orders(bits)
    def exchange(value, masks):
        perm = []
        for r in range(row_count):
            for k in range(col_count):
                perm.append((r * col_count + k, (r ^ masks[k % 2]) * col_count + k))
        return lax.ppermute(value, ("row", "col"), perm)

    held = piece[None]
    for start in range(0, bits, 2):
        groups = ((start,), (start + 1,), (start, start + 1)) if start + 1 < bits else ((start,),)
        parts = [held]
        for chosen in groups:
            masks = [sum(1 << order[p] for p in chosen) for order in (even, odd)]
            parts.append(exchange(held, masks))
        held = jnp.concatenate(parts, axis=0)

    def slot_of(owner, order_parity):
        diff = jnp.bitwise_xor(owner, me)
        slot_even = jnp.zeros_like(diff)
        slot_odd = jnp.zeros_like(diff)
        for position in range(bits):
            slot_even = slot_even + ((diff >> even[position]) & 1) * (1 << position)
            slot_odd = slot_odd + ((diff >> odd[position]) & 1) * (1 << position)
        return jnp.where(order_parity == 0, slot_even, slot_odd)

    return held, slot_of, parity


def shards(matrix, fill_mask, col_rows, inverses):
    col_index = lax.axis_index("col")
    row_index = lax.axis_index("row")
    row_count = lax.axis_size("row")
    col_count = lax.axis_size("col")
    local_rows, width = matrix.shape
    col_panels = width // PW
    block_rows = local_rows // RB
    local_slabs = local_rows // PW

    owner_row = col_rows // local_slabs
    piece, payload = prep_call(matrix, col_rows, fill_mask)
    held, slot_of, parity = gather_rows(piece, row_count, col_count)

    def wanted_of(group):
        own = group * col_panels + jnp.arange(col_panels, dtype=jnp.int32)
        return jnp.concatenate((own, jnp.full((1,), SECOND_COL * col_panels, jnp.int32)))

    def pick(pieces, wanted, order_parity):
        slots = slot_of(owner_row[wanted], order_parity)
        return jnp.take(pieces, slots, axis=0)

    wanted = wanted_of(col_index)
    if col_count == 2:
        swap = [(0, 1), (1, 0)]
        cols_a = payload
        cols_b = lax.ppermute(payload, "col", swap)
        pieces_a = pick(held, wanted, parity)
        for_partner = pick(held, wanted_of(1 - col_index), parity)
        pieces_b = lax.ppermute(for_partner, "col", swap)
    else:
        lead = lax.all_gather(payload, "col", axis=0, tiled=False)
        cols_a, cols_b = lead[FIRST_COL], lead[SECOND_COL]
        everyone = lax.all_gather(held, "col", axis=0, tiled=False)
        pieces_a = pick(everyone[FIRST_COL], wanted, FIRST_COL % 2)
        pieces_b = pick(everyone[SECOND_COL], wanted, SECOND_COL % 2)

    return factor_call(
        matrix, cols_a, cols_b, pieces_a, pieces_b, inverses, fill_mask, col_count == 2
    )


def prep_kernel(lead_ref, col_rows_ref, mask_ref, piece_ref, payload_ref):
    local_rows = lead_ref.shape[0]
    local_slabs = local_rows // PW
    block_rows = local_rows // RB
    row_index = lax.axis_index("row")
    place = jnp.int32(0)
    for c in range(col_rows_ref.shape[0]):
        entry = col_rows_ref[c]
        place = place + jnp.where(entry // local_slabs == row_index, entry % local_slabs, 0)
    place = jnp.minimum(place, local_slabs - 1)
    start = pl.multiple_of(place * PW, PW)
    flag = mask_ref[place // (RB // PW), 0]
    slab = lead_ref[pl.ds(start, PW), :].astype(jnp.float32)
    corner = (lax.broadcasted_iota(jnp.int32, (PW, PW), 0) == 0) & (
        lax.broadcasted_iota(jnp.int32, (PW, PW), 1) == 0
    )
    piece_ref[...] = jnp.where(corner & (flag == 0), jnp.nan, slab).astype(jnp.bfloat16)
    row_ids = lax.broadcasted_iota(jnp.int32, (MASK_ROWS, PW), 0)
    payload_ref[0:local_rows, :] = lead_ref[...]
    mask_rows = jnp.zeros((MASK_ROWS, PW), jnp.float32)
    for b in range(block_rows):
        mask_rows = jnp.where(row_ids == b, mask_ref[b, 0].astype(jnp.float32), mask_rows)
    payload_ref[local_rows : local_rows + MASK_ROWS, :] = mask_rows.astype(jnp.bfloat16)


def prep_call(matrix, col_rows, fill_mask):
    local_rows = matrix.shape[0]
    smem = pl.BlockSpec(memory_space=pltpu.SMEM)
    return pl.pallas_call(
        prep_kernel,
        out_shape=(
            jax.ShapeDtypeStruct((PW, PW), jnp.bfloat16),
            jax.ShapeDtypeStruct((local_rows + MASK_ROWS, PW), jnp.bfloat16),
        ),
        grid=(1,),
        in_specs=[pl.BlockSpec((local_rows, PW), lambda i: (0, 0)), smem, smem],
        out_specs=(
            pl.BlockSpec((PW, PW), lambda i: (0, 0)),
            pl.BlockSpec((local_rows + MASK_ROWS, PW), lambda i: (0, 0)),
        ),
        cost_estimate=pl.CostEstimate(
            flops=0, bytes_accessed=4 * local_rows * PW, transcendentals=0
        ),
    )(matrix, col_rows, fill_mask)


def factor_kernel(
    matrix_ref, cols_a_ref, cols_b_ref, pieces_a_ref, pieces_b_ref, inv_ref, mask_ref, out_ref, *, by_col
):
    local_rows, width = matrix_ref.shape
    col_panels = width // PW
    block_rows = local_rows // RB
    picks = pieces_a_ref.shape[0]
    col_index = lax.axis_index("col")
    swapped = (col_index != FIRST_COL) if by_col else False

    def dot(left, right):
        return jnp.dot(left, right, preferred_element_type=jnp.float32)

    def dot_t(left, right):
        return lax.dot_general(
            left, right, (((1,), (1,)), ((), ())), preferred_element_type=jnp.float32
        )

    def first_second(a_ref, b_ref, index):
        a_val, b_val = a_ref[index], b_ref[index]
        if not by_col:
            return a_val, b_val
        return jnp.where(swapped, b_val, a_val), jnp.where(swapped, a_val, b_val)

    upper = (
        lax.broadcasted_iota(jnp.int32, (PW, PW), 0) <= lax.broadcasted_iota(jnp.int32, (PW, PW), 1)
    )
    zero = jnp.zeros((PW, PW), jnp.bfloat16)
    upper_first = jnp.where(upper, inv_ref[0], zero)
    upper_second = jnp.where(upper, inv_ref[1], zero)

    slabs_first, slabs_second = first_second(
        pieces_a_ref, pieces_b_ref, (slice(None), slice(None), slice(None))
    )

    def filled(slabs):
        corner = slabs[:, 0:1, 0:1].astype(jnp.float32)
        return jnp.broadcast_to(corner == corner, slabs.shape)

    diag_first = jnp.where(
        filled(slabs_first),
        dot(slabs_first.reshape(picks * PW, PW), upper_first).reshape(picks, PW, PW),
        0.0,
    ).astype(jnp.bfloat16)
    pivot = diag_first[col_panels]
    own_first = diag_first[:col_panels].reshape(col_panels * PW, PW)
    diag_update = (
        slabs_second[:col_panels].reshape(col_panels * PW, PW).astype(jnp.float32)
        - dot_t(own_first, pivot)
    ).astype(jnp.bfloat16)
    diag_second = jnp.where(
        filled(slabs_second[:col_panels]),
        dot(diag_update, upper_second).reshape(col_panels, PW, PW),
        0.0,
    ).astype(jnp.bfloat16)

    cols_first, cols_second = first_second(cols_a_ref, cols_b_ref, slice(0, local_rows))
    rows_first, rows_second = first_second(
        cols_a_ref, cols_b_ref, slice(local_rows, local_rows + block_rows)
    )
    first_panel = (
        dot(cols_first, upper_first).reshape(block_rows, RB, PW)
        * rows_first.astype(jnp.float32)[:, None, :]
    ).astype(jnp.bfloat16).reshape(local_rows, PW)
    panel_update = (
        cols_second.astype(jnp.float32) - dot_t(first_panel, pivot)
    ).astype(jnp.bfloat16)
    second_panel = (
        dot(panel_update, upper_second).reshape(block_rows, RB, PW)
        * rows_second.astype(jnp.float32)[:, None, :]
    ).astype(jnp.bfloat16).reshape(local_rows, PW)
    both_panels = jnp.concatenate((first_panel, second_panel), axis=1)

    all_diag = jnp.concatenate(
        (diag_first[:col_panels].reshape(width, PW), diag_second.reshape(width, PW)), axis=1
    )
    product = dot_t(both_panels, all_diag)
    lane_panel = lax.broadcasted_iota(jnp.int32, (1, width), 1) // PW
    for b in range(block_rows):
        rows = slice(b * RB, (b + 1) * RB)
        scale = jnp.zeros((1, width), jnp.float32)
        for j in range(col_panels):
            scale = jnp.where(lane_panel == j, mask_ref[b, j].astype(jnp.float32), scale)
        schur = matrix_ref[rows, :].astype(jnp.float32) - product[rows]
        out_ref[rows, :] = (schur * scale).astype(jnp.bfloat16)
        lead = out_ref[rows, 0:PW]
        out_ref[rows, 0:PW] = jnp.where(
            col_index == FIRST_COL,
            first_panel[rows],
            jnp.where(col_index == SECOND_COL, second_panel[rows], lead),
        )


def factor_call(matrix, cols_a, cols_b, pieces_a, pieces_b, inverses, fill_mask, by_col):
    local_rows, width = matrix.shape
    vmem = pl.BlockSpec(memory_space=pltpu.VMEM)
    smem = pl.BlockSpec(memory_space=pltpu.SMEM)
    flops = 2 * local_rows * width * 2 * PW + 6 * local_rows * PW * PW
    return pl.pallas_call(
        functools.partial(factor_kernel, by_col=by_col),
        out_shape=jax.ShapeDtypeStruct((local_rows, width), jnp.bfloat16),
        in_specs=[vmem] * 6 + [smem],
        out_specs=vmem,
        cost_estimate=pl.CostEstimate(
            flops=flops, bytes_accessed=4 * local_rows * width, transcendentals=0
        ),
    )(matrix, cols_a, cols_b, pieces_a, pieces_b, inverses, fill_mask)


def solution(mesh):
    in_specs = (P("row", "col"), P("row", "col"), P(), P())
    out_specs = P("row", "col")
    return jax.shard_map(shards, mesh=mesh, in_specs=in_specs, out_specs=out_specs, check_vma=False)
```

```python
import functools

import jax
import jax.numpy as jnp
from jax import lax
from jax.experimental import pallas as pl
from jax.experimental.pallas import tpu as pltpu
from jax.sharding import PartitionSpec as P

RB = 256
PW = 128
FIRST_COL = 0
SECOND_COL = 1
MASK_ROWS = 16


def round_orders(bits):
    even = list(range(bits))[::-1]
    odd = list(even)
    for position in range(0, bits - 1, 2):
        odd[position], odd[position + 1] = odd[position + 1], odd[position]
    return even, odd


def gather_rows(piece, row_count, col_count, companion):
    me = lax.axis_index("row")
    parity = lax.axis_index("col") % 2
    bits = row_count.bit_length() - 1
    even, odd = round_orders(bits)
    def exchange(value, masks):
        perm = []
        for r in range(row_count):
            for k in range(col_count):
                perm.append((r * col_count + k, (r ^ masks[k % 2]) * col_count + k))
        return lax.ppermute(value, ("row", "col"), perm)

    held = piece[None]
    for start in range(0, bits, 2):
        groups = ((start,), (start + 1,), (start, start + 1)) if start + 1 < bits else ((start,),)
        parts = [held]
        for chosen in groups:
            masks = [sum(1 << order[p] for p in chosen) for order in (even, odd)]
            parts.append(exchange(held, masks))
        held = jnp.concatenate(parts, axis=0)
        if start == 0:
            held, companion = lax.optimization_barrier((held, companion))

    def slot_of(owner, order_parity):
        diff = jnp.bitwise_xor(owner, me)
        slot_even = jnp.zeros_like(diff)
        slot_odd = jnp.zeros_like(diff)
        for position in range(bits):
            slot_even = slot_even + ((diff >> even[position]) & 1) * (1 << position)
            slot_odd = slot_odd + ((diff >> odd[position]) & 1) * (1 << position)
        return jnp.where(order_parity == 0, slot_even, slot_odd)

    return held, slot_of, parity, companion


def shards(matrix, fill_mask, col_rows, inverses):
    col_index = lax.axis_index("col")
    row_index = lax.axis_index("row")
    row_count = lax.axis_size("row")
    col_count = lax.axis_size("col")
    local_rows, width = matrix.shape
    col_panels = width // PW
    block_rows = local_rows // RB
    local_slabs = local_rows // PW

    owner_row = col_rows // local_slabs
    piece, payload = prep_call(matrix, col_rows, fill_mask)
    if col_count == 2:
        swap = [(0, 1), (1, 0)]
        swapped_cols = lax.ppermute(payload, "col", swap)
    else:
        swapped_cols = payload
    held, slot_of, parity, swapped_cols = gather_rows(piece, row_count, col_count, swapped_cols)

    def wanted_of(group):
        own = group * col_panels + jnp.arange(col_panels, dtype=jnp.int32)
        return jnp.concatenate((own, jnp.full((1,), SECOND_COL * col_panels, jnp.int32)))

    def pick(pieces, wanted, order_parity):
        slots = slot_of(owner_row[wanted], order_parity)
        return jnp.take(pieces, slots, axis=0)

    wanted = wanted_of(col_index)
    if col_count == 2:
        cols_a = payload
        cols_b = swapped_cols
        pieces_a = pick(held, wanted, parity)
        for_partner = pick(held, wanted_of(1 - col_index), parity)
        pieces_b = lax.ppermute(for_partner, "col", swap)
    else:
        lead = lax.all_gather(payload, "col", axis=0, tiled=False)
        cols_a, cols_b = lead[FIRST_COL], lead[SECOND_COL]
        everyone = lax.all_gather(held, "col", axis=0, tiled=False)
        pieces_a = pick(everyone[FIRST_COL], wanted, FIRST_COL % 2)
        pieces_b = pick(everyone[SECOND_COL], wanted, SECOND_COL % 2)

    return factor_call(
        matrix, cols_a, cols_b, pieces_a, pieces_b, inverses, fill_mask, col_count == 2
    )


def prep_kernel(lead_ref, col_rows_ref, mask_ref, piece_ref, payload_ref):
    local_rows = lead_ref.shape[0]
    local_slabs = local_rows // PW
    block_rows = local_rows // RB
    row_index = lax.axis_index("row")
    place = jnp.int32(0)
    for c in range(col_rows_ref.shape[0]):
        entry = col_rows_ref[c]
        place = place + jnp.where(entry // local_slabs == row_index, entry % local_slabs, 0)
    place = jnp.minimum(place, local_slabs - 1)
    start = pl.multiple_of(place * PW, PW)
    flag = mask_ref[place // (RB // PW), 0]
    slab = lead_ref[pl.ds(start, PW), :].astype(jnp.float32)
    corner = (lax.broadcasted_iota(jnp.int32, (PW, PW), 0) == 0) & (
        lax.broadcasted_iota(jnp.int32, (PW, PW), 1) == 0
    )
    piece_ref[...] = jnp.where(corner & (flag == 0), jnp.nan, slab).astype(jnp.bfloat16)
    row_ids = lax.broadcasted_iota(jnp.int32, (MASK_ROWS, PW), 0)
    payload_ref[0:local_rows, :] = lead_ref[...]
    mask_rows = jnp.zeros((MASK_ROWS, PW), jnp.float32)
    for b in range(block_rows):
        mask_rows = jnp.where(row_ids == b, mask_ref[b, 0].astype(jnp.float32), mask_rows)
    payload_ref[local_rows : local_rows + MASK_ROWS, :] = mask_rows.astype(jnp.bfloat16)


def prep_call(matrix, col_rows, fill_mask):
    local_rows = matrix.shape[0]
    smem = pl.BlockSpec(memory_space=pltpu.SMEM)
    return pl.pallas_call(
        prep_kernel,
        out_shape=(
            jax.ShapeDtypeStruct((PW, PW), jnp.bfloat16),
            jax.ShapeDtypeStruct((local_rows + MASK_ROWS, PW), jnp.bfloat16),
        ),
        grid=(1,),
        in_specs=[pl.BlockSpec((local_rows, PW), lambda i: (0, 0)), smem, smem],
        out_specs=(
            pl.BlockSpec((PW, PW), lambda i: (0, 0)),
            pl.BlockSpec((local_rows + MASK_ROWS, PW), lambda i: (0, 0)),
        ),
        cost_estimate=pl.CostEstimate(
            flops=0, bytes_accessed=4 * local_rows * PW, transcendentals=0
        ),
    )(matrix, col_rows, fill_mask)


def factor_kernel(
    matrix_ref, cols_a_ref, cols_b_ref, pieces_a_ref, pieces_b_ref, inv_ref, mask_ref, out_ref, *, by_col
):
    local_rows, width = matrix_ref.shape
    col_panels = width // PW
    block_rows = local_rows // RB
    picks = pieces_a_ref.shape[0]
    col_index = lax.axis_index("col")
    swapped = (col_index != FIRST_COL) if by_col else False

    def dot(left, right):
        return jnp.dot(left, right, preferred_element_type=jnp.float32)

    def dot_t(left, right):
        return lax.dot_general(
            left, right, (((1,), (1,)), ((), ())), preferred_element_type=jnp.float32
        )

    def first_second(a_ref, b_ref, index):
        a_val, b_val = a_ref[index], b_ref[index]
        if not by_col:
            return a_val, b_val
        return jnp.where(swapped, b_val, a_val), jnp.where(swapped, a_val, b_val)

    upper = (
        lax.broadcasted_iota(jnp.int32, (PW, PW), 0) <= lax.broadcasted_iota(jnp.int32, (PW, PW), 1)
    )
    zero = jnp.zeros((PW, PW), jnp.bfloat16)
    upper_first = jnp.where(upper, inv_ref[0], zero)
    upper_second = jnp.where(upper, inv_ref[1], zero)

    slabs_first, slabs_second = first_second(
        pieces_a_ref, pieces_b_ref, (slice(None), slice(None), slice(None))
    )

    def filled(slabs):
        corner = slabs[:, 0:1, 0:1].astype(jnp.float32)
        return jnp.broadcast_to(corner == corner, slabs.shape)

    diag_first = jnp.where(
        filled(slabs_first),
        dot(slabs_first.reshape(picks * PW, PW), upper_first).reshape(picks, PW, PW),
        0.0,
    ).astype(jnp.bfloat16)
    pivot = diag_first[col_panels]
    own_first = diag_first[:col_panels].reshape(col_panels * PW, PW)
    diag_update = (
        slabs_second[:col_panels].reshape(col_panels * PW, PW).astype(jnp.float32)
        - dot_t(own_first, pivot)
    ).astype(jnp.bfloat16)
    diag_second = jnp.where(
        filled(slabs_second[:col_panels]),
        dot(diag_update, upper_second).reshape(col_panels, PW, PW),
        0.0,
    ).astype(jnp.bfloat16)

    cols_first, cols_second = first_second(cols_a_ref, cols_b_ref, slice(0, local_rows))
    rows_first, rows_second = first_second(
        cols_a_ref, cols_b_ref, slice(local_rows, local_rows + block_rows)
    )
    first_panel = (
        dot(cols_first, upper_first).reshape(block_rows, RB, PW)
        * rows_first.astype(jnp.float32)[:, None, :]
    ).astype(jnp.bfloat16).reshape(local_rows, PW)
    panel_update = (
        cols_second.astype(jnp.float32) - dot_t(first_panel, pivot)
    ).astype(jnp.bfloat16)
    second_panel = (
        dot(panel_update, upper_second).reshape(block_rows, RB, PW)
        * rows_second.astype(jnp.float32)[:, None, :]
    ).astype(jnp.bfloat16).reshape(local_rows, PW)
    both_panels = jnp.concatenate((first_panel, second_panel), axis=1)

    all_diag = jnp.concatenate(
        (diag_first[:col_panels].reshape(width, PW), diag_second.reshape(width, PW)), axis=1
    )
    product = dot_t(both_panels, all_diag)
    lane_panel = lax.broadcasted_iota(jnp.int32, (1, width), 1) // PW
    for b in range(block_rows):
        rows = slice(b * RB, (b + 1) * RB)
        scale = jnp.zeros((1, width), jnp.float32)
        for j in range(col_panels):
            scale = jnp.where(lane_panel == j, mask_ref[b, j].astype(jnp.float32), scale)
        schur = matrix_ref[rows, :].astype(jnp.float32) - product[rows]
        out_ref[rows, :] = (schur * scale).astype(jnp.bfloat16)
        lead = out_ref[rows, 0:PW]
        out_ref[rows, 0:PW] = jnp.where(
            col_index == FIRST_COL,
            first_panel[rows],
            jnp.where(col_index == SECOND_COL, second_panel[rows], lead),
        )


def factor_call(matrix, cols_a, cols_b, pieces_a, pieces_b, inverses, fill_mask, by_col):
    local_rows, width = matrix.shape
    vmem = pl.BlockSpec(memory_space=pltpu.VMEM)
    smem = pl.BlockSpec(memory_space=pltpu.SMEM)
    flops = 2 * local_rows * width * 2 * PW + 6 * local_rows * PW * PW
    return pl.pallas_call(
        functools.partial(factor_kernel, by_col=by_col),
        out_shape=jax.ShapeDtypeStruct((local_rows, width), jnp.bfloat16),
        in_specs=[vmem] * 6 + [smem],
        out_specs=vmem,
        cost_estimate=pl.CostEstimate(
            flops=flops, bytes_accessed=4 * local_rows * width, transcendentals=0
        ),
    )(matrix, cols_a, cols_b, pieces_a, pieces_b, inverses, fill_mask)


def solution(mesh):
    in_specs = (P("row", "col"), P("row", "col"), P(), P())
    out_specs = P("row", "col")
    return jax.shard_map(shards, mesh=mesh, in_specs=in_specs, out_specs=out_specs, check_vma=False)
```

```python
import functools

import jax
import jax.numpy as jnp
from jax import lax
from jax.experimental import pallas as pl
from jax.experimental.pallas import tpu as pltpu
from jax.sharding import PartitionSpec as P

RB = 256
PW = 128
FIRST_COL = 0
SECOND_COL = 1
MASK_ROWS = 16


def round_orders(bits):
    even = list(range(bits))[::-1]
    odd = list(even)
    for position in range(0, bits - 1, 2):
        odd[position], odd[position + 1] = odd[position + 1], odd[position]
    return even, odd


def gather_rows(piece, row_count, col_count):
    me = lax.axis_index("row")
    parity = lax.axis_index("col") % 2
    bits = row_count.bit_length() - 1
    even, odd = round_orders(bits)
    def exchange(value, masks):
        perm = []
        for r in range(row_count):
            for k in range(col_count):
                perm.append((r * col_count + k, (r ^ masks[k % 2]) * col_count + k))
        return lax.ppermute(value, ("row", "col"), perm)

    held = piece[None]
    for start in range(0, bits, 2):
        groups = ((start,), (start + 1,), (start, start + 1)) if start + 1 < bits else ((start,),)
        parts = [held]
        for chosen in groups:
            masks = [sum(1 << order[p] for p in chosen) for order in (even, odd)]
            parts.append(exchange(held, masks))
        held = jnp.concatenate(parts, axis=0)

    def slot_of(owner, order_parity):
        diff = jnp.bitwise_xor(owner, me)
        slot_even = jnp.zeros_like(diff)
        slot_odd = jnp.zeros_like(diff)
        for position in range(bits):
            slot_even = slot_even + ((diff >> even[position]) & 1) * (1 << position)
            slot_odd = slot_odd + ((diff >> odd[position]) & 1) * (1 << position)
        return jnp.where(order_parity == 0, slot_even, slot_odd)

    return held, slot_of, parity


def shards(matrix, fill_mask, col_rows, inverses):
    col_index = lax.axis_index("col")
    row_index = lax.axis_index("row")
    row_count = lax.axis_size("row")
    col_count = lax.axis_size("col")
    local_rows, width = matrix.shape
    col_panels = width // PW
    block_rows = local_rows // RB
    local_slabs = local_rows // PW

    owner_row = col_rows // local_slabs
    piece, payload = prep_call(matrix, col_rows, fill_mask)
    held, slot_of, parity = gather_rows(piece, row_count, col_count)

    def wanted_of(group):
        own = group * col_panels + jnp.arange(col_panels, dtype=jnp.int32)
        return jnp.concatenate((own, jnp.full((1,), SECOND_COL * col_panels, jnp.int32)))

    def pick(pieces, wanted, order_parity):
        slots = slot_of(owner_row[wanted], order_parity)
        return jnp.take(pieces, slots, axis=0)

    wanted = wanted_of(col_index)
    if col_count == 2:
        swap = [(0, 1), (1, 0)]
        cols_a = payload
        cols_b = lax.ppermute(payload, "col", swap)
        pieces_a = pick(held, wanted, parity)
        for_partner = pick(held, wanted_of(1 - col_index), parity)
        pieces_b = lax.ppermute(for_partner, "col", swap)
    else:
        lead = lax.all_gather(payload, "col", axis=0, tiled=False)
        cols_a, cols_b = lead[FIRST_COL], lead[SECOND_COL]
        everyone = lax.all_gather(held, "col", axis=0, tiled=False)
        pieces_a = pick(everyone[FIRST_COL], wanted, FIRST_COL % 2)
        pieces_b = pick(everyone[SECOND_COL], wanted, SECOND_COL % 2)

    return factor_call(
        matrix, cols_a, cols_b, pieces_a, pieces_b, inverses, fill_mask, col_count == 2
    )


def prep_kernel(matrix_hbm, col_rows_ref, mask_ref, piece_ref, slab_ref, sem):
    local_rows = matrix_hbm.shape[0]
    local_slabs = local_rows // PW
    row_index = lax.axis_index("row")
    place = jnp.int32(0)
    for c in range(col_rows_ref.shape[0]):
        entry = col_rows_ref[c]
        place = place + jnp.where(entry // local_slabs == row_index, entry % local_slabs, 0)
    place = jnp.minimum(place, local_slabs - 1)
    start = pl.multiple_of(place * PW, PW)
    copy = pltpu.make_async_copy(matrix_hbm.at[pl.ds(start, PW), pl.ds(0, PW)], slab_ref, sem.at[0])
    copy.start()
    flag = mask_ref[place // (RB // PW), 0]
    corner = (lax.broadcasted_iota(jnp.int32, (PW, PW), 0) == 0) & (
        lax.broadcasted_iota(jnp.int32, (PW, PW), 1) == 0
    )
    copy.wait()
    slab = slab_ref[...].astype(jnp.float32)
    piece_ref[...] = jnp.where(corner & (flag == 0), jnp.nan, slab).astype(jnp.bfloat16)


def prep_call(matrix, col_rows, fill_mask):
    local_rows = matrix.shape[0]
    block_rows = local_rows // RB
    smem = pl.BlockSpec(memory_space=pltpu.SMEM)
    piece = pl.pallas_call(
        prep_kernel,
        out_shape=jax.ShapeDtypeStruct((PW, PW), jnp.bfloat16),
        in_specs=[pl.BlockSpec(memory_space=pltpu.HBM), smem, smem],
        out_specs=pl.BlockSpec(memory_space=pltpu.VMEM),
        scratch_shapes=[pltpu.VMEM((PW, PW), jnp.bfloat16), pltpu.SemaphoreType.DMA((1,))],
        cost_estimate=pl.CostEstimate(flops=0, bytes_accessed=4 * PW * PW, transcendentals=0),
    )(matrix, col_rows, fill_mask)
    mask_rows = jnp.zeros((MASK_ROWS, PW), jnp.bfloat16)
    mask_rows = mask_rows.at[:block_rows].set(
        jnp.broadcast_to(fill_mask[:, 0:1].astype(jnp.bfloat16), (block_rows, PW))
    )
    payload = jnp.concatenate((matrix[:, :PW], mask_rows), axis=0)
    return piece, payload


def factor_kernel(
    matrix_ref, cols_a_ref, cols_b_ref, pieces_a_ref, pieces_b_ref, inv_ref, mask_ref, out_ref, *, by_col
):
    local_rows, width = matrix_ref.shape
    col_panels = width // PW
    block_rows = local_rows // RB
    picks = pieces_a_ref.shape[0]
    col_index = lax.axis_index("col")
    swapped = (col_index != FIRST_COL) if by_col else False

    def dot(left, right):
        return jnp.dot(left, right, preferred_element_type=jnp.float32)

    def dot_t(left, right):
        return lax.dot_general(
            left, right, (((1,), (1,)), ((), ())), preferred_element_type=jnp.float32
        )

    def first_second(a_ref, b_ref, index):
        a_val, b_val = a_ref[index], b_ref[index]
        if not by_col:
            return a_val, b_val
        return jnp.where(swapped, b_val, a_val), jnp.where(swapped, a_val, b_val)

    upper = (
        lax.broadcasted_iota(jnp.int32, (PW, PW), 0) <= lax.broadcasted_iota(jnp.int32, (PW, PW), 1)
    )
    zero = jnp.zeros((PW, PW), jnp.bfloat16)
    upper_first = jnp.where(upper, inv_ref[0], zero)
    upper_second = jnp.where(upper, inv_ref[1], zero)

    slabs_first, slabs_second = first_second(
        pieces_a_ref, pieces_b_ref, (slice(None), slice(None), slice(None))
    )

    def filled(slabs):
        corner = slabs[:, 0:1, 0:1].astype(jnp.float32)
        return jnp.broadcast_to(corner == corner, slabs.shape)

    diag_first = jnp.where(
        filled(slabs_first),
        dot(slabs_first.reshape(picks * PW, PW), upper_first).reshape(picks, PW, PW),
        0.0,
    ).astype(jnp.bfloat16)
    pivot = diag_first[col_panels]
    own_first = diag_first[:col_panels].reshape(col_panels * PW, PW)
    diag_update = (
        slabs_second[:col_panels].reshape(col_panels * PW, PW).astype(jnp.float32)
        - dot_t(own_first, pivot)
    ).astype(jnp.bfloat16)
    diag_second = jnp.where(
        filled(slabs_second[:col_panels]),
        dot(diag_update, upper_second).reshape(col_panels, PW, PW),
        0.0,
    ).astype(jnp.bfloat16)

    cols_first, cols_second = first_second(cols_a_ref, cols_b_ref, slice(0, local_rows))
    rows_first, rows_second = first_second(
        cols_a_ref, cols_b_ref, slice(local_rows, local_rows + block_rows)
    )
    first_panel = (
        dot(cols_first, upper_first).reshape(block_rows, RB, PW)
        * rows_first.astype(jnp.float32)[:, None, :]
    ).astype(jnp.bfloat16).reshape(local_rows, PW)
    panel_update = (
        cols_second.astype(jnp.float32) - dot_t(first_panel, pivot)
    ).astype(jnp.bfloat16)
    second_panel = (
        dot(panel_update, upper_second).reshape(block_rows, RB, PW)
        * rows_second.astype(jnp.float32)[:, None, :]
    ).astype(jnp.bfloat16).reshape(local_rows, PW)
    both_panels = jnp.concatenate((first_panel, second_panel), axis=1)

    all_diag = jnp.concatenate(
        (diag_first[:col_panels].reshape(width, PW), diag_second.reshape(width, PW)), axis=1
    )
    product = dot_t(both_panels, all_diag)
    lane_panel = lax.broadcasted_iota(jnp.int32, (1, width), 1) // PW
    for b in range(block_rows):
        rows = slice(b * RB, (b + 1) * RB)
        scale = jnp.zeros((1, width), jnp.float32)
        for j in range(col_panels):
            scale = jnp.where(lane_panel == j, mask_ref[b, j].astype(jnp.float32), scale)
        schur = matrix_ref[rows, :].astype(jnp.float32) - product[rows]
        out_ref[rows, :] = (schur * scale).astype(jnp.bfloat16)
        lead = out_ref[rows, 0:PW]
        out_ref[rows, 0:PW] = jnp.where(
            col_index == FIRST_COL,
            first_panel[rows],
            jnp.where(col_index == SECOND_COL, second_panel[rows], lead),
        )


def factor_call(matrix, cols_a, cols_b, pieces_a, pieces_b, inverses, fill_mask, by_col):
    local_rows, width = matrix.shape
    vmem = pl.BlockSpec(memory_space=pltpu.VMEM)
    smem = pl.BlockSpec(memory_space=pltpu.SMEM)
    flops = 2 * local_rows * width * 2 * PW + 6 * local_rows * PW * PW
    return pl.pallas_call(
        functools.partial(factor_kernel, by_col=by_col),
        out_shape=jax.ShapeDtypeStruct((local_rows, width), jnp.bfloat16),
        in_specs=[vmem] * 6 + [smem],
        out_specs=vmem,
        cost_estimate=pl.CostEstimate(
            flops=flops, bytes_accessed=4 * local_rows * width, transcendentals=0
        ),
    )(matrix, cols_a, cols_b, pieces_a, pieces_b, inverses, fill_mask)


def solution(mesh):
    in_specs = (P("row", "col"), P("row", "col"), P(), P())
    out_specs = P("row", "col")
    return jax.shard_map(shards, mesh=mesh, in_specs=in_specs, out_specs=out_specs, check_vma=False)
```

```python
import functools

import jax
import jax.numpy as jnp
from jax import lax
from jax.experimental import pallas as pl
from jax.experimental.pallas import tpu as pltpu
from jax.sharding import PartitionSpec as P

RB = 256
PW = 128
FIRST_COL = 0
SECOND_COL = 1
MASK_ROWS = 16


def round_orders(bits):
    even = list(range(bits))[::-1]
    odd = list(even)
    for position in range(0, bits - 1, 2):
        odd[position], odd[position + 1] = odd[position + 1], odd[position]
    return even, odd


def gather_rows(piece, row_count, col_count):
    me = lax.axis_index("row")
    parity = lax.axis_index("col") % 2
    bits = row_count.bit_length() - 1
    even, odd = round_orders(bits)
    def exchange(value, masks):
        perm = []
        for r in range(row_count):
            for k in range(col_count):
                perm.append((r * col_count + k, (r ^ masks[k % 2]) * col_count + k))
        return lax.ppermute(value, ("row", "col"), perm)

    held = piece[None]
    for start in range(0, bits, 2):
        groups = ((start,), (start + 1,), (start, start + 1)) if start + 1 < bits else ((start,),)
        parts = [held]
        for chosen in groups:
            masks = [sum(1 << order[p] for p in chosen) for order in (even, odd)]
            parts.append(exchange(held, masks))
        joined = jnp.zeros((len(parts) * held.shape[0],) + held.shape[1:], held.dtype)
        for index, part in enumerate(parts):
            joined = lax.dynamic_update_slice_in_dim(joined, part, index * held.shape[0], 0)
        held = joined

    def slot_of(owner, order_parity):
        diff = jnp.bitwise_xor(owner, me)
        slot_even = jnp.zeros_like(diff)
        slot_odd = jnp.zeros_like(diff)
        for position in range(bits):
            slot_even = slot_even + ((diff >> even[position]) & 1) * (1 << position)
            slot_odd = slot_odd + ((diff >> odd[position]) & 1) * (1 << position)
        return jnp.where(order_parity == 0, slot_even, slot_odd)

    return held, slot_of, parity


def shards(matrix, fill_mask, col_rows, inverses):
    col_index = lax.axis_index("col")
    row_index = lax.axis_index("row")
    row_count = lax.axis_size("row")
    col_count = lax.axis_size("col")
    local_rows, width = matrix.shape
    col_panels = width // PW
    block_rows = local_rows // RB
    local_slabs = local_rows // PW

    owner_row = col_rows // local_slabs
    piece, payload = prep_call(matrix, col_rows, fill_mask)
    held, slot_of, parity = gather_rows(piece, row_count, col_count)

    def wanted_of(group):
        own = group * col_panels + jnp.arange(col_panels, dtype=jnp.int32)
        return jnp.concatenate((own, jnp.full((1,), SECOND_COL * col_panels, jnp.int32)))

    def pick(pieces, wanted, order_parity):
        slots = slot_of(owner_row[wanted], order_parity)
        return jnp.take(pieces, slots, axis=0)

    wanted = wanted_of(col_index)
    if col_count == 2:
        swap = [(0, 1), (1, 0)]
        cols_a = payload
        cols_b = lax.ppermute(payload, "col", swap)
        pieces_a = pick(held, wanted, parity)
        for_partner = pick(held, wanted_of(1 - col_index), parity)
        pieces_b = lax.ppermute(for_partner, "col", swap)
    else:
        lead = lax.all_gather(payload, "col", axis=0, tiled=False)
        cols_a, cols_b = lead[FIRST_COL], lead[SECOND_COL]
        everyone = lax.all_gather(held, "col", axis=0, tiled=False)
        pieces_a = pick(everyone[FIRST_COL], wanted, FIRST_COL % 2)
        pieces_b = pick(everyone[SECOND_COL], wanted, SECOND_COL % 2)

    return factor_call(
        matrix, cols_a, cols_b, pieces_a, pieces_b, inverses, fill_mask, col_count == 2
    )


def prep_kernel(matrix_hbm, col_rows_ref, mask_ref, piece_ref, slab_ref, sem):
    local_rows = matrix_hbm.shape[0]
    local_slabs = local_rows // PW
    row_index = lax.axis_index("row")
    place = jnp.int32(0)
    for c in range(col_rows_ref.shape[0]):
        entry = col_rows_ref[c]
        place = place + jnp.where(entry // local_slabs == row_index, entry % local_slabs, 0)
    place = jnp.minimum(place, local_slabs - 1)
    start = pl.multiple_of(place * PW, PW)
    copy = pltpu.make_async_copy(matrix_hbm.at[pl.ds(start, PW), pl.ds(0, PW)], slab_ref, sem.at[0])
    copy.start()
    flag = mask_ref[place // (RB // PW), 0]
    corner = (lax.broadcasted_iota(jnp.int32, (PW, PW), 0) == 0) & (
        lax.broadcasted_iota(jnp.int32, (PW, PW), 1) == 0
    )
    copy.wait()
    slab = slab_ref[...].astype(jnp.float32)
    piece_ref[...] = jnp.where(corner & (flag == 0), jnp.nan, slab).astype(jnp.bfloat16)


def prep_call(matrix, col_rows, fill_mask):
    local_rows = matrix.shape[0]
    block_rows = local_rows // RB
    smem = pl.BlockSpec(memory_space=pltpu.SMEM)
    piece = pl.pallas_call(
        prep_kernel,
        out_shape=jax.ShapeDtypeStruct((PW, PW), jnp.bfloat16),
        in_specs=[pl.BlockSpec(memory_space=pltpu.HBM), smem, smem],
        out_specs=pl.BlockSpec(memory_space=pltpu.VMEM),
        scratch_shapes=[pltpu.VMEM((PW, PW), jnp.bfloat16), pltpu.SemaphoreType.DMA((1,))],
        cost_estimate=pl.CostEstimate(flops=0, bytes_accessed=4 * PW * PW, transcendentals=0),
    )(matrix, col_rows, fill_mask)
    mask_rows = jnp.zeros((MASK_ROWS, PW), jnp.bfloat16)
    mask_rows = mask_rows.at[:block_rows].set(
        jnp.broadcast_to(fill_mask[:, 0:1].astype(jnp.bfloat16), (block_rows, PW))
    )
    payload = jnp.concatenate((matrix[:, :PW], mask_rows), axis=0)
    return piece, payload


def factor_kernel(
    matrix_ref, cols_a_ref, cols_b_ref, pieces_a_ref, pieces_b_ref, inv_ref, mask_ref, out_ref, *, by_col
):
    local_rows, width = matrix_ref.shape
    col_panels = width // PW
    block_rows = local_rows // RB
    picks = pieces_a_ref.shape[0]
    col_index = lax.axis_index("col")
    swapped = (col_index != FIRST_COL) if by_col else False

    def dot(left, right):
        return jnp.dot(left, right, preferred_element_type=jnp.float32)

    def dot_t(left, right):
        return lax.dot_general(
            left, right, (((1,), (1,)), ((), ())), preferred_element_type=jnp.float32
        )

    def first_second(a_ref, b_ref, index):
        a_val, b_val = a_ref[index], b_ref[index]
        if not by_col:
            return a_val, b_val
        return jnp.where(swapped, b_val, a_val), jnp.where(swapped, a_val, b_val)

    upper = (
        lax.broadcasted_iota(jnp.int32, (PW, PW), 0) <= lax.broadcasted_iota(jnp.int32, (PW, PW), 1)
    )
    zero = jnp.zeros((PW, PW), jnp.bfloat16)
    upper_first = jnp.where(upper, inv_ref[0], zero)
    upper_second = jnp.where(upper, inv_ref[1], zero)

    slabs_first, slabs_second = first_second(
        pieces_a_ref, pieces_b_ref, (slice(None), slice(None), slice(None))
    )

    def filled(slabs):
        corner = slabs[:, 0:1, 0:1].astype(jnp.float32)
        return jnp.broadcast_to(corner == corner, slabs.shape)

    diag_first = jnp.where(
        filled(slabs_first),
        dot(slabs_first.reshape(picks * PW, PW), upper_first).reshape(picks, PW, PW),
        0.0,
    ).astype(jnp.bfloat16)
    pivot = diag_first[col_panels]
    own_first = diag_first[:col_panels].reshape(col_panels * PW, PW)
    diag_update = (
        slabs_second[:col_panels].reshape(col_panels * PW, PW).astype(jnp.float32)
        - dot_t(own_first, pivot)
    ).astype(jnp.bfloat16)
    diag_second = jnp.where(
        filled(slabs_second[:col_panels]),
        dot(diag_update, upper_second).reshape(col_panels, PW, PW),
        0.0,
    ).astype(jnp.bfloat16)

    cols_first, cols_second = first_second(cols_a_ref, cols_b_ref, slice(0, local_rows))
    rows_first, rows_second = first_second(
        cols_a_ref, cols_b_ref, slice(local_rows, local_rows + block_rows)
    )
    first_panel = (
        dot(cols_first, upper_first).reshape(block_rows, RB, PW)
        * rows_first.astype(jnp.float32)[:, None, :]
    ).astype(jnp.bfloat16).reshape(local_rows, PW)
    panel_update = (
        cols_second.astype(jnp.float32) - dot_t(first_panel, pivot)
    ).astype(jnp.bfloat16)
    second_panel = (
        dot(panel_update, upper_second).reshape(block_rows, RB, PW)
        * rows_second.astype(jnp.float32)[:, None, :]
    ).astype(jnp.bfloat16).reshape(local_rows, PW)
    both_panels = jnp.concatenate((first_panel, second_panel), axis=1)

    all_diag = jnp.concatenate(
        (diag_first[:col_panels].reshape(width, PW), diag_second.reshape(width, PW)), axis=1
    )
    product = dot_t(both_panels, all_diag)
    lane_panel = lax.broadcasted_iota(jnp.int32, (1, width), 1) // PW
    for b in range(block_rows):
        rows = slice(b * RB, (b + 1) * RB)
        scale = jnp.zeros((1, width), jnp.float32)
        for j in range(col_panels):
            scale = jnp.where(lane_panel == j, mask_ref[b, j].astype(jnp.float32), scale)
        schur = matrix_ref[rows, :].astype(jnp.float32) - product[rows]
        out_ref[rows, :] = (schur * scale).astype(jnp.bfloat16)
        lead = out_ref[rows, 0:PW]
        out_ref[rows, 0:PW] = jnp.where(
            col_index == FIRST_COL,
            first_panel[rows],
            jnp.where(col_index == SECOND_COL, second_panel[rows], lead),
        )


def factor_call(matrix, cols_a, cols_b, pieces_a, pieces_b, inverses, fill_mask, by_col):
    local_rows, width = matrix.shape
    vmem = pl.BlockSpec(memory_space=pltpu.VMEM)
    smem = pl.BlockSpec(memory_space=pltpu.SMEM)
    flops = 2 * local_rows * width * 2 * PW + 6 * local_rows * PW * PW
    return pl.pallas_call(
        functools.partial(factor_kernel, by_col=by_col),
        out_shape=jax.ShapeDtypeStruct((local_rows, width), jnp.bfloat16),
        in_specs=[vmem] * 6 + [smem],
        out_specs=vmem,
        cost_estimate=pl.CostEstimate(
            flops=flops, bytes_accessed=4 * local_rows * width, transcendentals=0
        ),
    )(matrix, cols_a, cols_b, pieces_a, pieces_b, inverses, fill_mask)


def solution(mesh):
    in_specs = (P("row", "col"), P("row", "col"), P(), P())
    out_specs = P("row", "col")
    return jax.shard_map(shards, mesh=mesh, in_specs=in_specs, out_specs=out_specs, check_vma=False)
```
